512 devices in a mesh: rev: 8 (over z_lo, x), bin: 64 (over y, z_hi, core).
Axes of the slice: x: 4, y: 8, z: 8 (z_hi: 4, z_lo: 2; z = z_hi * 2 + z_lo), core: 2. Of those that a mesh axis runs over, the one named last changes fastest.
Arguments:
- snapshots: float32 [8, 512, 3, 24, 8, 128], P('rev', 'bin'), may hold values from -6 to 6
- phase_index: int32 [8, 512], P('rev', 'bin'), may hold values from 0 to 255, as said below
Outputs:
- stress_terms: float32 [4, 6, 256, 24, 8, 128], P(None, None, 'bin', 'rev')
- mean_velocity: float32 [3, 256, 24, 8, 128], P(None, 'bin', 'rev')
The draws below stay inside these ranges and needn't reach their ends.
Inputs may be any that keep to these rules, and one draw needn't show every extreme that they name: `phase_index`: the rows b * 8 to (b + 1) * 8 - 1 of a revolution shard name bins b * 4 to (b + 1) * 4 - 1 only, and each of these bins at least once.
All inputs are finite; a program needn't handle non-finite values.
Results may differ from the reference program's by a relative error of at most 0.00017.
Values sent between devices are 32-bit elements; how exact they have to be, the bound alone decides.
No kernel may reach another device: no remote copies, remote signals or barrier semaphores. Data moves between devices by JAX's collectives and lax.ppermute only.
A program may use at most 64 MiB of HBM per device.

```python
import jax
import jax.numpy as jnp
from jax import lax

PHASES = 256
NY = 8
NZ = 128
PB_DEV = 4
SNAP_DEV = 8
SNAPS = 512
NX = 24
N_REV = 8
N_BIN = 64


def draw_phase_index(key, part):
    random_bins = jax.random.randint(jax.random.fold_in(key, 3), (N_REV, N_BIN, SNAP_DEV), 0, PB_DEV).astype(jnp.int32)
    position = jnp.arange(SNAP_DEV, dtype=jnp.int32)
    base = jnp.where(position[None, None, :] < PB_DEV, (position % PB_DEV)[None, None, :], random_bins)
    keys = jax.random.split(jax.random.fold_in(key, 7), N_REV * N_BIN)
    orders = jax.vmap(lambda single: jax.random.permutation(single, SNAP_DEV))(keys)
    orders = orders.reshape(N_REV, N_BIN, SNAP_DEV).astype(jnp.int32)
    local_bins = jnp.take_along_axis(base, orders, axis=2)
    first_bin = (jnp.arange(N_BIN, dtype=jnp.int32) * PB_DEV)[None, :, None]
    return (local_bins + first_bin).reshape(N_REV, N_BIN * SNAP_DEV).astype(jnp.int32)


def levels(rng, extent, cuts, low, largest):
    loudness = 1.0
    for axis_at, parts in cuts:
        draws = jax.random.uniform(jax.random.fold_in(jax.random.fold_in(rng, 6), axis_at), (parts,), jnp.float32, low / len(cuts), largest / len(cuts))
        loudness = loudness * jnp.repeat(jnp.exp(draws), extent[axis_at] // parts).reshape((-1,) + (1,) * (len(extent) - 1 - axis_at))
    return loudness


def normal_values(key, dims, spread, bound, shards=(), held_as=jnp.bfloat16):
    entries = jax.random.normal(key, dims, jnp.float32) * spread
    if len(shards) > 0:
        entries = levels(key, dims, shards, -0.22, 0.18) * entries
    return jnp.clip(entries, min=-bound, max=bound).astype(held_as)


def setup_inputs(seed: int = 0) -> dict:
    key_of = jax.random.split(jax.random.key(seed), 3)
    snapshots = normal_values(key_of[0], (N_REV, SNAPS, 3, NX, NY, NZ), 1.0, 6.0, ((0, 8), (1, 64)), jnp.float32)
    phase_index = draw_phase_index(jax.random.fold_in(key_of[2], 71), 0)
    return dict(snapshots=snapshots, phase_index=phase_index)


viscosity = 0.2
stress_pairs = ((0, 0), (0, 1), (0, 2), (1, 1), (1, 2), (2, 2))


def pair_index(first, second):
    low, high = min(first, second), max(first, second)
    return stress_pairs.index((low, high))


def moment_fields(frame):
    vel_x, vel_y, vel_z = frame[0], frame[1], frame[2]
    return jnp.stack([jnp.ones_like(vel_x), vel_x, vel_y, vel_z, vel_x * vel_x, vel_x * vel_y,
                      vel_x * vel_z, vel_y * vel_y, vel_y * vel_z, vel_z * vel_z])


def first_diff(field, axis):
    def shifted(amount):
        return jnp.roll(field, -amount, axis)
    return 0.75 * (shifted(1) - shifted(-1)) - 0.15 * (shifted(2) - shifted(-2)) + (shifted(3) - shifted(-3)) / 60.0


def second_diff(field, axis):
    def shifted(amount):
        return jnp.roll(field, -amount, axis)
    return (-49.0 / 18.0 * field + 1.5 * (shifted(1) + shifted(-1)) - 0.15 * (shifted(2) + shifted(-2))
            + (shifted(3) + shifted(-3)) / 90.0)


def reference(snapshots, phase_index):
    frames = snapshots.reshape((-1, 3, NX, NY, NZ))
    bin_list = phase_index.reshape(-1).astype(jnp.int32)

    def accumulate(running, entry):
        frame, which = entry
        return running.at[which].add(moment_fields(frame)), None

    sums, _ = lax.scan(accumulate, jnp.zeros((PHASES, 10, NX, NY, NZ), jnp.float32), (frames, bin_list))
    samples = sums[:, 0]
    velocity = [sums[:, 1 + comp] / samples for comp in range(3)]
    stresses = [sums[:, 4 + slot] / samples - velocity[pair[0]] * velocity[pair[1]]
                for slot, pair in enumerate(stress_pairs)]
    grad_u = [[first_diff(velocity[comp], 1 + dim) for dim in range(3)] for comp in range(3)]
    unsteady, convect, produce, diffuse = [], [], [], []
    for slot, pair in enumerate(stress_pairs):
        first, second = pair
        stress = stresses[slot]
        unsteady.append(first_diff(stress, 0))
        grads = [first_diff(stress, 1 + dim) for dim in range(3)]
        convect.append(velocity[0] * grads[0] + velocity[1] * grads[1] + velocity[2] * grads[2])
        summed = jnp.zeros_like(stress)
        for dim in range(3):
            summed = summed + stresses[pair_index(first, dim)] * grad_u[second][dim] + stresses[pair_index(second, dim)] * grad_u[first][dim]
        produce.append(-summed)
        diffuse.append(viscosity * (second_diff(stress, 1) + second_diff(stress, 2) + second_diff(stress, 3)))
    terms_all = jnp.stack([jnp.stack(unsteady), jnp.stack(convect), jnp.stack(produce), jnp.stack(diffuse)])
    return terms_all, jnp.stack(velocity)
```

```python
import jax
import jax.numpy as jnp
from jax import lax
from jax.experimental import pallas as pl
from jax.experimental.pallas import tpu as pltpu
from jax.sharding import PartitionSpec as P

PHASES = 256

viscosity = 0.2
stress_pairs = ((0, 0), (0, 1), (0, 2), (1, 1), (1, 2), (2, 2))


def pair_index(first, second):
    low, high = (min(first, second), max(first, second))
    return stress_pairs.index((low, high))


def bin_kernel(bins_ref, counts_ref, x_ref, o_ref, acc_ref):
    snaps, _, planes = x_ref.shape[0], x_ref.shape[1], x_ref.shape[2]
    bins = acc_ref.shape[0]
    acc_ref[...] = jnp.zeros(acc_ref.shape, jnp.float32)

    def body(s, carry):
        b = bins_ref[s]
        for p in range(planes):
            u = x_ref[s, 0, p]
            v = x_ref[s, 1, p]
            w = x_ref[s, 2, p]
            moments = (u, v, w, u * u, u * v, u * w, v * v, v * w, w * w)
            for k in range(9):
                acc_ref[b, k, p] = acc_ref[b, k, p] + moments[k]
        return carry

    lax.fori_loop(0, snaps, body, 0)

    for b in range(bins):
        count = counts_ref[b]
        for p in range(planes):
            vel = [acc_ref[b, c, p] / count for c in range(3)]
            for c in range(3):
                o_ref[c, b, p] = vel[c]
            for slot, (i, j) in enumerate(stress_pairs):
                o_ref[3 + slot, b, p] = acc_ref[b, 3 + slot, p] / count - vel[i] * vel[j]


def binned_fields(frames, local_bins, counts):
    snaps, _, planes, ny, nz = frames.shape
    bins = counts.shape[0]
    return pl.pallas_call(
        bin_kernel,
        out_shape=jax.ShapeDtypeStruct((9, bins, planes, ny, nz), jnp.float32),
        in_specs=[
            pl.BlockSpec(memory_space=pltpu.SMEM),
            pl.BlockSpec(memory_space=pltpu.SMEM),
            pl.BlockSpec(memory_space=pltpu.VMEM),
        ],
        out_specs=pl.BlockSpec(memory_space=pltpu.VMEM),
        scratch_shapes=[pltpu.VMEM((bins, 9, planes, ny, nz), jnp.float32)],
        cost_estimate=pl.CostEstimate(
            flops=snaps * planes * ny * nz * 15,
            bytes_accessed=frames.size * 4 + 9 * bins * planes * ny * nz * 4,
            transcendentals=0,
        ),
    )(local_bins, counts, frames)


def first_diff(shifted):
    return (
        0.75 * (shifted(1) - shifted(-1))
        - 0.15 * (shifted(2) - shifted(-2))
        + (shifted(3) - shifted(-3)) / 60.0
    )


def second_diff(shifted, centre):
    return (
        -49.0 / 18.0 * centre
        + 1.5 * (shifted(1) + shifted(-1))
        - 0.15 * (shifted(2) + shifted(-2))
        + (shifted(3) + shifted(-3)) / 90.0
    )


def ring(axis, step):
    count = lax.axis_size(axis)
    return [(i, (i + step) % count) for i in range(count)]


def finish_terms(fields):
    bins_dev, planes = fields.shape[1], fields.shape[2]
    from_left = lax.ppermute(fields, "rev", ring("rev", 1))
    from_right = lax.ppermute(fields, "rev", ring("rev", -1))
    stress_all = fields[3:]
    from_prev = lax.ppermute(stress_all[:, bins_dev - 3 :], "bin", ring("bin", 1))
    from_next = lax.ppermute(stress_all[:, :3], "bin", ring("bin", -1))
    padded_x = jnp.concatenate([from_left, fields, from_right], axis=2)
    padded_p = jnp.concatenate([from_prev, stress_all, from_next], axis=1)

    velocity = [fields[c] for c in range(3)]
    stresses = [fields[3 + m] for m in range(6)]

    def along(component, dim, centre):
        if dim == 0:
            source = padded_x[component]
            return lambda amount: source[:, planes + amount : 2 * planes + amount]
        if dim == 3:
            source = padded_p[component - 3]
            return lambda amount: source[3 + amount : 3 + amount + bins_dev]
        return lambda amount: jnp.roll(centre, -amount, dim + 1)

    grad_u = [
        [first_diff(along(comp, dim, velocity[comp])) for dim in range(3)] for comp in range(3)
    ]
    unsteady, convect, produce, diffuse = ([], [], [], [])
    for slot, pair in enumerate(stress_pairs):
        first, second = pair
        stress = stresses[slot]
        unsteady.append(first_diff(along(3 + slot, 3, stress)))
        grads = [first_diff(along(3 + slot, dim, stress)) for dim in range(3)]
        convect.append(velocity[0] * grads[0] + velocity[1] * grads[1] + velocity[2] * grads[2])
        summed = jnp.zeros_like(stress)
        for dim in range(3):
            summed = (
                summed
                + stresses[pair_index(first, dim)] * grad_u[second][dim]
                + stresses[pair_index(second, dim)] * grad_u[first][dim]
            )
        produce.append(-summed)
        diffuse.append(
            viscosity
            * (
                second_diff(along(3 + slot, 0, stress), stress)
                + second_diff(along(3 + slot, 1, stress), stress)
                + second_diff(along(3 + slot, 2, stress), stress)
            )
        )
    terms_all = jnp.stack(
        [jnp.stack(unsteady), jnp.stack(convect), jnp.stack(produce), jnp.stack(diffuse)]
    )
    return terms_all, fields[:3]


def shards(snapshots, phase_index):
    bins_dev = PHASES // lax.axis_size("bin")
    frames = lax.all_to_all(snapshots[0], "rev", 2, 0, tiled=True)
    phases = lax.all_gather(phase_index[0], "rev", tiled=True)
    local_bins = jnp.clip(phases - lax.axis_index("bin") * bins_dev, 0, bins_dev - 1)
    one_hot = local_bins[None, :] == jnp.arange(bins_dev, dtype=jnp.int32)[:, None]
    counts = jnp.sum(one_hot.astype(jnp.float32), axis=1)
    fields = binned_fields(frames, local_bins, counts)
    return finish_terms(fields)


def solution(mesh):
    in_specs = (P("rev", "bin", None, None, None, None), P("rev", "bin"))
    out_specs = (P(None, None, "bin", "rev", None, None), P(None, "bin", "rev", None, None))
    return jax.shard_map(shards, mesh=mesh, in_specs=in_specs, out_specs=out_specs, check_vma=False)
```

```python
import jax
import jax.numpy as jnp
from jax import lax
from jax.experimental import pallas as pl
from jax.experimental.pallas import tpu as pltpu
from jax.sharding import PartitionSpec as P

PHASES = 256

viscosity = 0.2
stress_pairs = ((0, 0), (0, 1), (0, 2), (1, 1), (1, 2), (2, 2))


def pair_index(first, second):
    low, high = (min(first, second), max(first, second))
    return stress_pairs.index((low, high))


def bin_kernel(bins_ref, counts_ref, x_ref, o_ref, acc_ref):
    bins, _, planes = acc_ref.shape[0], acc_ref.shape[1], acc_ref.shape[2]
    per_src = (x_ref.shape[1] - 1) // (3 * planes)
    snaps = x_ref.shape[0] * per_src
    acc_ref[...] = jnp.zeros(acc_ref.shape, jnp.float32)

    def body(s, carry):
        b = bins_ref[s]
        src = s // per_src
        base = (s % per_src) * (3 * planes)
        for p in range(planes):
            u = x_ref[src, base + p]
            v = x_ref[src, base + planes + p]
            w = x_ref[src, base + 2 * planes + p]
            moments = (u, v, w, u * u, u * v, u * w, v * v, v * w, w * w)
            for k in range(9):
                acc_ref[b, k, p] = acc_ref[b, k, p] + moments[k]
        return carry

    lax.fori_loop(0, snaps, body, 0)

    for b in range(bins):
        count = counts_ref[b]
        for p in range(planes):
            vel = [acc_ref[b, c, p] / count for c in range(3)]
            for c in range(3):
                o_ref[c, b, p] = vel[c]
            for slot, (i, j) in enumerate(stress_pairs):
                o_ref[3 + slot, b, p] = acc_ref[b, 3 + slot, p] / count - vel[i] * vel[j]


def binned_fields(received, local_bins, counts, planes):
    n_src, rows, ny, nz = received.shape
    bins = counts.shape[0]
    snaps = local_bins.shape[0]
    return pl.pallas_call(
        bin_kernel,
        out_shape=jax.ShapeDtypeStruct((9, bins, planes, ny, nz), jnp.float32),
        in_specs=[
            pl.BlockSpec(memory_space=pltpu.SMEM),
            pl.BlockSpec(memory_space=pltpu.SMEM),
            pl.BlockSpec(memory_space=pltpu.VMEM),
        ],
        out_specs=pl.BlockSpec(memory_space=pltpu.VMEM),
        scratch_shapes=[pltpu.VMEM((bins, 9, planes, ny, nz), jnp.float32)],
        cost_estimate=pl.CostEstimate(
            flops=snaps * planes * ny * nz * 15,
            bytes_accessed=received.size * 4 + 9 * bins * planes * ny * nz * 4,
            transcendentals=0,
        ),
    )(local_bins, counts, received)


def first_diff(shifted):
    return (
        0.75 * (shifted(1) - shifted(-1))
        - 0.15 * (shifted(2) - shifted(-2))
        + (shifted(3) - shifted(-3)) / 60.0
    )


def second_diff(shifted, centre):
    return (
        -49.0 / 18.0 * centre
        + 1.5 * (shifted(1) + shifted(-1))
        - 0.15 * (shifted(2) + shifted(-2))
        + (shifted(3) + shifted(-3)) / 90.0
    )


def ring(axis, step):
    count = lax.axis_size(axis)
    return [(i, (i + step) % count) for i in range(count)]


def finish_terms(fields):
    bins_dev, planes = fields.shape[1], fields.shape[2]
    from_left = lax.ppermute(fields, "rev", ring("rev", 1))
    from_right = lax.ppermute(fields, "rev", ring("rev", -1))
    stress_all = fields[3:]
    from_prev = lax.ppermute(stress_all[:, bins_dev - 3 :], "bin", ring("bin", 1))
    from_next = lax.ppermute(stress_all[:, :3], "bin", ring("bin", -1))
    padded_x = jnp.concatenate([from_left, fields, from_right], axis=2)
    padded_p = jnp.concatenate([from_prev, stress_all, from_next], axis=1)

    velocity = [fields[c] for c in range(3)]
    stresses = [fields[3 + m] for m in range(6)]

    def along(component, dim, centre):
        if dim == 0:
            source = padded_x[component]
            return lambda amount: source[:, planes + amount : 2 * planes + amount]
        if dim == 3:
            source = padded_p[component - 3]
            return lambda amount: source[3 + amount : 3 + amount + bins_dev]
        return lambda amount: jnp.roll(centre, -amount, dim + 1)

    grad_u = [
        [first_diff(along(comp, dim, velocity[comp])) for dim in range(3)] for comp in range(3)
    ]
    unsteady, convect, produce, diffuse = ([], [], [], [])
    for slot, pair in enumerate(stress_pairs):
        first, second = pair
        stress = stresses[slot]
        unsteady.append(first_diff(along(3 + slot, 3, stress)))
        grads = [first_diff(along(3 + slot, dim, stress)) for dim in range(3)]
        convect.append(velocity[0] * grads[0] + velocity[1] * grads[1] + velocity[2] * grads[2])
        summed = jnp.zeros_like(stress)
        for dim in range(3):
            summed = (
                summed
                + stresses[pair_index(first, dim)] * grad_u[second][dim]
                + stresses[pair_index(second, dim)] * grad_u[first][dim]
            )
        produce.append(-summed)
        diffuse.append(
            viscosity
            * (
                second_diff(along(3 + slot, 0, stress), stress)
                + second_diff(along(3 + slot, 1, stress), stress)
                + second_diff(along(3 + slot, 2, stress), stress)
            )
        )
    terms_all = jnp.stack(
        [jnp.stack(unsteady), jnp.stack(convect), jnp.stack(produce), jnp.stack(diffuse)]
    )
    return terms_all, fields[:3]


def shards(snapshots, phase_index):
    bins_dev = PHASES // lax.axis_size("bin")
    n_rev = lax.axis_size("rev")
    frames = snapshots[0]
    snaps, comps, nx, ny, nz = frames.shape
    planes = nx // n_rev
    by_dest = frames.reshape(snaps, comps, n_rev, planes, ny, nz)
    by_dest = jnp.transpose(by_dest, (2, 0, 1, 3, 4, 5)).reshape(n_rev, snaps * comps * planes, ny, nz)
    phase_row = jnp.pad(phase_index[0].astype(jnp.float32), (0, nz - snaps))
    phase_slab = jnp.broadcast_to(phase_row[None, None, None, :], (n_rev, 1, ny, nz))
    payload = jnp.concatenate([by_dest, phase_slab], axis=1)
    received = lax.all_to_all(payload, "rev", 0, 0, tiled=True)
    phases = received[:, -1, 0, :snaps].reshape(-1).astype(jnp.int32)
    local_bins = jnp.clip(phases - lax.axis_index("bin") * bins_dev, 0, bins_dev - 1)
    one_hot = local_bins[None, :] == jnp.arange(bins_dev, dtype=jnp.int32)[:, None]
    counts = jnp.sum(one_hot.astype(jnp.float32), axis=1)
    fields = binned_fields(received, local_bins, counts, planes)
    return finish_terms(fields)


def solution(mesh):
    in_specs = (P("rev", "bin", None, None, None, None), P("rev", "bin"))
    out_specs = (P(None, None, "bin", "rev", None, None), P(None, "bin", "rev", None, None))
    return jax.shard_map(shards, mesh=mesh, in_specs=in_specs, out_specs=out_specs, check_vma=False)
```

```python
import jax
import jax.numpy as jnp
from jax import lax
from jax.experimental import pallas as pl
from jax.experimental.pallas import tpu as pltpu
from jax.sharding import PartitionSpec as P

PHASES = 256
HALO = 3

viscosity = 0.2
stress_pairs = ((0, 0), (0, 1), (0, 2), (1, 1), (1, 2), (2, 2))


def pair_index(first, second):
    low, high = (min(first, second), max(first, second))
    return stress_pairs.index((low, high))


def bin_kernel(bins_ref, counts_ref, x_ref, o_ref, head_ref, tail_ref, acc_ref):
    bins, _, planes = acc_ref.shape[0], acc_ref.shape[1], acc_ref.shape[2]
    per_src = (x_ref.shape[1] - 1) // (3 * planes)
    snaps = x_ref.shape[0] * per_src
    acc_ref[...] = jnp.zeros(acc_ref.shape, jnp.float32)

    def body(s, carry):
        b = bins_ref[s]
        src = s // per_src
        base = (s % per_src) * (3 * planes)
        for p in range(planes):
            u = x_ref[src, base + p]
            v = x_ref[src, base + planes + p]
            w = x_ref[src, base + 2 * planes + p]
            moments = (u, v, w, u * u, u * v, u * w, v * v, v * w, w * w)
            for k in range(9):
                acc_ref[b, k, p] = acc_ref[b, k, p] + moments[k]
        return carry

    lax.fori_loop(0, snaps, body, 0)

    for b in range(bins):
        count = counts_ref[b]
        for p in range(planes):
            vel = [acc_ref[b, c, p] / count for c in range(3)]
            for c in range(3):
                o_ref[c, b, p] = vel[c]
            for slot, (i, j) in enumerate(stress_pairs):
                stress = acc_ref[b, 3 + slot, p] / count - vel[i] * vel[j]
                o_ref[3 + slot, b, p] = stress
                if b < HALO:
                    head_ref[slot, b, p] = stress
                if b >= bins - HALO:
                    tail_ref[slot, b - (bins - HALO), p] = stress


def binned_fields(received, local_bins, counts, planes):
    n_src, rows, ny, nz = received.shape
    bins = counts.shape[0]
    snaps = local_bins.shape[0]
    return pl.pallas_call(
        bin_kernel,
        out_shape=(
            jax.ShapeDtypeStruct((9, bins, planes, ny, nz), jnp.float32),
            jax.ShapeDtypeStruct((6, HALO, planes, ny, nz), jnp.float32),
            jax.ShapeDtypeStruct((6, HALO, planes, ny, nz), jnp.float32),
        ),
        in_specs=[
            pl.BlockSpec(memory_space=pltpu.SMEM),
            pl.BlockSpec(memory_space=pltpu.SMEM),
            pl.BlockSpec(memory_space=pltpu.VMEM),
        ],
        out_specs=(
            pl.BlockSpec(memory_space=pltpu.VMEM),
            pl.BlockSpec(memory_space=pltpu.VMEM),
            pl.BlockSpec(memory_space=pltpu.VMEM),
        ),
        scratch_shapes=[pltpu.VMEM((bins, 9, planes, ny, nz), jnp.float32)],
        cost_estimate=pl.CostEstimate(
            flops=snaps * planes * ny * nz * 15,
            bytes_accessed=received.size * 4 + 9 * bins * planes * ny * nz * 4,
            transcendentals=0,
        ),
    )(local_bins, counts, received)


def first_diff(shifted):
    return (
        0.75 * (shifted(1) - shifted(-1))
        - 0.15 * (shifted(2) - shifted(-2))
        + (shifted(3) - shifted(-3)) / 60.0
    )


def second_diff(shifted, centre):
    return (
        -49.0 / 18.0 * centre
        + 1.5 * (shifted(1) + shifted(-1))
        - 0.15 * (shifted(2) + shifted(-2))
        + (shifted(3) + shifted(-3)) / 90.0
    )


def ring(axis, step):
    count = lax.axis_size(axis)
    return [(i, (i + step) % count) for i in range(count)]


def stencil_kernel(f_ref, fl_ref, fr_ref, rp_ref, rn_ref, terms_ref, vel_ref):
    _, bins, planes, ny, nz = f_ref.shape

    def at(comp, b, x):
        if 0 <= x < planes:
            if 0 <= b < bins:
                return f_ref[comp, b, x]
            if b < 0:
                return rp_ref[comp - 3, b + HALO, x]
            return rn_ref[comp - 3, b - bins, x]
        if x < 0:
            return fl_ref[comp, b, x + planes]
        return fr_ref[comp, b, x - planes]

    def rolled(value, axis, size):
        table = {k: pltpu.roll(value, (-k) % size, axis) for k in (1, 2, 3, -1, -2, -3)}
        return lambda amount: table[amount]

    for b in range(bins):
        for x in range(planes):
            velocity = [f_ref[c, b, x] for c in range(3)]
            stresses = [f_ref[3 + m, b, x] for m in range(6)]
            for c in range(3):
                vel_ref[c, b, x] = velocity[c]
            grad_u = [
                [
                    first_diff(lambda k, c=c: at(c, b, x + k)),
                    first_diff(rolled(velocity[c], 0, ny)),
                    first_diff(rolled(velocity[c], 1, nz)),
                ]
                for c in range(3)
            ]
            for slot, (first, second) in enumerate(stress_pairs):
                comp = 3 + slot
                stress = stresses[slot]
                along_x = lambda k, comp=comp: at(comp, b, x + k)
                along_y = rolled(stress, 0, ny)
                along_z = rolled(stress, 1, nz)
                terms_ref[0, slot, b, x] = first_diff(lambda k, comp=comp: at(comp, b + k, x))
                grads = [first_diff(along_x), first_diff(along_y), first_diff(along_z)]
                terms_ref[1, slot, b, x] = (
                    velocity[0] * grads[0] + velocity[1] * grads[1] + velocity[2] * grads[2]
                )
                summed = jnp.zeros_like(stress)
                for dim in range(3):
                    summed = (
                        summed
                        + stresses[pair_index(first, dim)] * grad_u[second][dim]
                        + stresses[pair_index(second, dim)] * grad_u[first][dim]
                    )
                terms_ref[2, slot, b, x] = -summed
                terms_ref[3, slot, b, x] = viscosity * (
                    second_diff(along_x, stress)
                    + second_diff(along_y, stress)
                    + second_diff(along_z, stress)
                )


def finish_terms(fields, head, tail):
    _, bins_dev, planes, ny, nz = fields.shape
    from_left = lax.ppermute(fields, "rev", ring("rev", 1))
    from_right = lax.ppermute(fields, "rev", ring("rev", -1))
    from_prev = lax.ppermute(tail, "bin", ring("bin", 1))
    from_next = lax.ppermute(head, "bin", ring("bin", -1))
    cells = bins_dev * planes * ny * nz
    vmem = pl.BlockSpec(memory_space=pltpu.VMEM)
    return pl.pallas_call(
        stencil_kernel,
        out_shape=(
            jax.ShapeDtypeStruct((4, 6, bins_dev, planes, ny, nz), jnp.float32),
            jax.ShapeDtypeStruct((3, bins_dev, planes, ny, nz), jnp.float32),
        ),
        in_specs=[vmem] * 5,
        out_specs=(vmem, vmem),
        cost_estimate=pl.CostEstimate(
            flops=cells * 700,
            bytes_accessed=(3 * fields.size + 2 * head.size + 27 * cells) * 4,
            transcendentals=0,
        ),
    )(fields, from_left, from_right, from_prev, from_next)


def shards(snapshots, phase_index):
    bins_dev = PHASES // lax.axis_size("bin")
    n_rev = lax.axis_size("rev")
    frames = snapshots[0]
    snaps, comps, nx, ny, nz = frames.shape
    planes = nx // n_rev
    by_dest = frames.reshape(snaps, comps, n_rev, planes, ny, nz)
    by_dest = jnp.transpose(by_dest, (2, 0, 1, 3, 4, 5)).reshape(n_rev, snaps * comps * planes, ny, nz)
    phase_row = jnp.pad(phase_index[0].astype(jnp.float32), (0, nz - snaps))
    phase_slab = jnp.broadcast_to(phase_row[None, None, None, :], (n_rev, 1, ny, nz))
    payload = jnp.concatenate([by_dest, phase_slab], axis=1)
    received = lax.all_to_all(payload, "rev", 0, 0, tiled=True)
    phases = received[:, -1, 0, :snaps].reshape(-1).astype(jnp.int32)
    local_bins = jnp.clip(phases - lax.axis_index("bin") * bins_dev, 0, bins_dev - 1)
    one_hot = local_bins[None, :] == jnp.arange(bins_dev, dtype=jnp.int32)[:, None]
    counts = jnp.sum(one_hot.astype(jnp.float32), axis=1)
    fields, head, tail = binned_fields(received, local_bins, counts, planes)
    return finish_terms(fields, head, tail)


def solution(mesh):
    in_specs = (P("rev", "bin", None, None, None, None), P("rev", "bin"))
    out_specs = (P(None, None, "bin", "rev", None, None), P(None, "bin", "rev", None, None))
    return jax.shard_map(shards, mesh=mesh, in_specs=in_specs, out_specs=out_specs, check_vma=False)
```

```python
import jax
import jax.numpy as jnp
from jax import lax
from jax.experimental import pallas as pl
from jax.experimental.pallas import tpu as pltpu
from jax.sharding import PartitionSpec as P

PHASES = 256
HALO = 3

viscosity = 0.2
stress_pairs = ((0, 0), (0, 1), (0, 2), (1, 1), (1, 2), (2, 2))


def pair_index(first, second):
    low, high = (min(first, second), max(first, second))
    return stress_pairs.index((low, high))


def bin_kernel(bins_ref, x_ref, o_ref, head_ref, tail_ref, order_ref, bounds_ref):
    bins, planes, ny, nz = o_ref.shape[1], o_ref.shape[2], o_ref.shape[3], o_ref.shape[4]
    per_src = (x_ref.shape[1] - 1) // (3 * planes)
    snaps = x_ref.shape[0] * per_src

    position = jnp.int32(0)
    for b in range(bins):
        bounds_ref[b] = position

        def place(s, pos, b=b):
            order_ref[pos] = s
            return pos + (bins_ref[s] == b).astype(jnp.int32)

        position = lax.fori_loop(0, snaps, place, position)
    bounds_ref[bins] = position

    for b in range(bins):

        def gather(i, carry):
            s = order_ref[i]
            src = s // per_src
            base = (s % per_src) * (3 * planes)
            sums, count = carry
            new = []
            for p in range(planes):
                u = x_ref[src, base + p]
                v = x_ref[src, base + planes + p]
                w = x_ref[src, base + 2 * planes + p]
                moments = (u, v, w, u * u, u * v, u * w, v * v, v * w, w * w)
                new.extend(sums[9 * p + k] + moments[k] for k in range(9))
            return tuple(new), count + 1.0

        zero = jnp.zeros((ny, nz), jnp.float32)
        sums, count = lax.fori_loop(
            bounds_ref[b], bounds_ref[b + 1], gather, (tuple([zero] * (9 * planes)), zero)
        )
        for p in range(planes):
            vel = [sums[9 * p + c] / count for c in range(3)]
            for c in range(3):
                o_ref[c, b, p] = vel[c]
            for slot, (i, j) in enumerate(stress_pairs):
                stress = sums[9 * p + 3 + slot] / count - vel[i] * vel[j]
                o_ref[3 + slot, b, p] = stress
                if b < HALO:
                    head_ref[slot, b, p] = stress
                if b >= bins - HALO:
                    tail_ref[slot, b - (bins - HALO), p] = stress


def binned_fields(received, local_bins, bins, planes):
    n_src, rows, ny, nz = received.shape
    snaps = local_bins.shape[0]
    vmem = pl.BlockSpec(memory_space=pltpu.VMEM)
    return pl.pallas_call(
        bin_kernel,
        out_shape=(
            jax.ShapeDtypeStruct((9, bins, planes, ny, nz), jnp.float32),
            jax.ShapeDtypeStruct((6, HALO, planes, ny, nz), jnp.float32),
            jax.ShapeDtypeStruct((6, HALO, planes, ny, nz), jnp.float32),
        ),
        in_specs=[pl.BlockSpec(memory_space=pltpu.SMEM), vmem],
        out_specs=(vmem, vmem, vmem),
        scratch_shapes=[pltpu.SMEM((snaps + 1,), jnp.int32), pltpu.SMEM((bins + 1,), jnp.int32)],
        cost_estimate=pl.CostEstimate(
            flops=snaps * planes * ny * nz * 15,
            bytes_accessed=received.size * 4 + 9 * bins * planes * ny * nz * 4,
            transcendentals=0,
        ),
    )(local_bins, received)


def first_diff(shifted):
    return (
        0.75 * (shifted(1) - shifted(-1))
        - 0.15 * (shifted(2) - shifted(-2))
        + (shifted(3) - shifted(-3)) / 60.0
    )


def second_diff(shifted, centre):
    return (
        -49.0 / 18.0 * centre
        + 1.5 * (shifted(1) + shifted(-1))
        - 0.15 * (shifted(2) + shifted(-2))
        + (shifted(3) + shifted(-3)) / 90.0
    )


def ring(axis, step):
    count = lax.axis_size(axis)
    return [(i, (i + step) % count) for i in range(count)]


def stencil_kernel(f_ref, fl_ref, fr_ref, rp_ref, rn_ref, terms_ref, vel_ref):
    _, bins, planes, ny, nz = f_ref.shape

    def at(comp, b, x):
        if 0 <= x < planes:
            if 0 <= b < bins:
                return f_ref[comp, b, x]
            if b < 0:
                return rp_ref[comp - 3, b + HALO, x]
            return rn_ref[comp - 3, b - bins, x]
        if x < 0:
            return fl_ref[comp, b, x + planes]
        return fr_ref[comp, b, x - planes]

    def rolled(value, axis, size):
        table = {k: pltpu.roll(value, (-k) % size, axis) for k in (1, 2, 3, -1, -2, -3)}
        return lambda amount: table[amount]

    for b in range(bins):
        for x in range(planes):
            velocity = [f_ref[c, b, x] for c in range(3)]
            stresses = [f_ref[3 + m, b, x] for m in range(6)]
            for c in range(3):
                vel_ref[c, b, x] = velocity[c]
            grad_u = [
                [
                    first_diff(lambda k, c=c: at(c, b, x + k)),
                    first_diff(rolled(velocity[c], 0, ny)),
                    first_diff(rolled(velocity[c], 1, nz)),
                ]
                for c in range(3)
            ]
            for slot, (first, second) in enumerate(stress_pairs):
                comp = 3 + slot
                stress = stresses[slot]
                along_x = lambda k, comp=comp: at(comp, b, x + k)
                along_y = rolled(stress, 0, ny)
                along_z = rolled(stress, 1, nz)
                terms_ref[0, slot, b, x] = first_diff(lambda k, comp=comp: at(comp, b + k, x))
                grads = [first_diff(along_x), first_diff(along_y), first_diff(along_z)]
                terms_ref[1, slot, b, x] = (
                    velocity[0] * grads[0] + velocity[1] * grads[1] + velocity[2] * grads[2]
                )
                summed = jnp.zeros_like(stress)
                for dim in range(3):
                    summed = (
                        summed
                        + stresses[pair_index(first, dim)] * grad_u[second][dim]
                        + stresses[pair_index(second, dim)] * grad_u[first][dim]
                    )
                terms_ref[2, slot, b, x] = -summed
                terms_ref[3, slot, b, x] = viscosity * (
                    second_diff(along_x, stress)
                    + second_diff(along_y, stress)
                    + second_diff(along_z, stress)
                )


def finish_terms(fields, head, tail):
    _, bins_dev, planes, ny, nz = fields.shape
    from_left = lax.ppermute(fields, "rev", ring("rev", 1))
    from_right = lax.ppermute(fields, "rev", ring("rev", -1))
    from_prev = lax.ppermute(tail, "bin", ring("bin", 1))
    from_next = lax.ppermute(head, "bin", ring("bin", -1))
    cells = bins_dev * planes * ny * nz
    vmem = pl.BlockSpec(memory_space=pltpu.VMEM)
    return pl.pallas_call(
        stencil_kernel,
        out_shape=(
            jax.ShapeDtypeStruct((4, 6, bins_dev, planes, ny, nz), jnp.float32),
            jax.ShapeDtypeStruct((3, bins_dev, planes, ny, nz), jnp.float32),
        ),
        in_specs=[vmem] * 5,
        out_specs=(vmem, vmem),
        cost_estimate=pl.CostEstimate(
            flops=cells * 700,
            bytes_accessed=(3 * fields.size + 2 * head.size + 27 * cells) * 4,
            transcendentals=0,
        ),
    )(fields, from_left, from_right, from_prev, from_next)


def shards(snapshots, phase_index):
    bins_dev = PHASES // lax.axis_size("bin")
    n_rev = lax.axis_size("rev")
    frames = snapshots[0]
    snaps, comps, nx, ny, nz = frames.shape
    planes = nx // n_rev
    by_dest = frames.reshape(snaps, comps, n_rev, planes, ny, nz)
    by_dest = jnp.transpose(by_dest, (2, 0, 1, 3, 4, 5)).reshape(n_rev, snaps * comps * planes, ny, nz)
    phase_row = jnp.pad(phase_index[0].astype(jnp.float32), (0, nz - snaps))
    phase_slab = jnp.broadcast_to(phase_row[None, None, None, :], (n_rev, 1, ny, nz))
    payload = jnp.concatenate([by_dest, phase_slab], axis=1)
    received = lax.all_to_all(payload, "rev", 0, 0, tiled=True)
    phases = received[:, -1, 0, :snaps].reshape(-1).astype(jnp.int32)
    local_bins = jnp.clip(phases - lax.axis_index("bin") * bins_dev, 0, bins_dev - 1)
    fields, head, tail = binned_fields(received, local_bins, bins_dev, planes)
    return finish_terms(fields, head, tail)


def solution(mesh):
    in_specs = (P("rev", "bin", None, None, None, None), P("rev", "bin"))
    out_specs = (P(None, None, "bin", "rev", None, None), P(None, "bin", "rev", None, None))
    return jax.shard_map(shards, mesh=mesh, in_specs=in_specs, out_specs=out_specs, check_vma=False)
```

```python
import jax
import jax.numpy as jnp
from jax import lax
from jax.experimental import pallas as pl
from jax.experimental.pallas import tpu as pltpu
from jax.sharding import PartitionSpec as P

PHASES = 256
HALO = 3

viscosity = 0.2
stress_pairs = ((0, 0), (0, 1), (0, 2), (1, 1), (1, 2), (2, 2))


def pair_index(first, second):
    low, high = (min(first, second), max(first, second))
    return stress_pairs.index((low, high))


def bin_kernel(bins_ref, counts_ref, x_ref, o_ref, head_ref, tail_ref, acc_ref):
    bins, _, planes = acc_ref.shape[0], acc_ref.shape[1], acc_ref.shape[2]
    per_src = (x_ref.shape[1] - 1) // (3 * planes)
    snaps = x_ref.shape[0] * per_src
    acc_ref[...] = jnp.zeros(acc_ref.shape, jnp.float32)

    def body(s, carry):
        b = bins_ref[s]
        src = s // per_src
        base = (s % per_src) * (3 * planes)
        for p in range(planes):
            u = x_ref[src, base + p]
            v = x_ref[src, base + planes + p]
            w = x_ref[src, base + 2 * planes + p]
            moments = (u, v, w, u * u, u * v, u * w, v * v, v * w, w * w)
            for k in range(9):
                acc_ref[b, k, p] = acc_ref[b, k, p] + moments[k]
        return carry

    lax.fori_loop(0, snaps, body, 0)

    for b in range(bins):
        count = counts_ref[b]
        for p in range(planes):
            vel = [acc_ref[b, c, p] / count for c in range(3)]
            for c in range(3):
                o_ref[c, b, p] = vel[c]
            for slot, (i, j) in enumerate(stress_pairs):
                stress = acc_ref[b, 3 + slot, p] / count - vel[i] * vel[j]
                o_ref[3 + slot, b, p] = stress
                if b < HALO:
                    head_ref[slot, b, p] = stress
                if b >= bins - HALO:
                    tail_ref[slot, b - (bins - HALO), p] = stress


def binned_fields(received, local_bins, counts, planes):
    n_src, rows, ny, nz = received.shape
    bins = counts.shape[0]
    snaps = local_bins.shape[0]
    return pl.pallas_call(
        bin_kernel,
        out_shape=(
            jax.ShapeDtypeStruct((9, bins, planes, ny, nz), jnp.float32),
            jax.ShapeDtypeStruct((6, HALO, planes, ny, nz), jnp.float32),
            jax.ShapeDtypeStruct((6, HALO, planes, ny, nz), jnp.float32),
        ),
        in_specs=[
            pl.BlockSpec(memory_space=pltpu.SMEM),
            pl.BlockSpec(memory_space=pltpu.SMEM),
            pl.BlockSpec(memory_space=pltpu.VMEM),
        ],
        out_specs=(
            pl.BlockSpec(memory_space=pltpu.VMEM),
            pl.BlockSpec(memory_space=pltpu.VMEM),
            pl.BlockSpec(memory_space=pltpu.VMEM),
        ),
        scratch_shapes=[pltpu.VMEM((bins, 9, planes, ny, nz), jnp.float32)],
        cost_estimate=pl.CostEstimate(
            flops=snaps * planes * ny * nz * 15,
            bytes_accessed=received.size * 4 + 9 * bins * planes * ny * nz * 4,
            transcendentals=0,
        ),
    )(local_bins, counts, received)


def pack_kernel(phase_ref, x_ref, o_ref):
    snaps, comps, _, ny, nz = x_ref.shape
    n_dest, rows = o_ref.shape[0], o_ref.shape[1]
    planes = (rows - 1) // (snaps * comps)
    for d in range(n_dest):
        for s in range(snaps):
            for c in range(comps):
                o_ref[d, pl.ds((s * comps + c) * planes, planes)] = x_ref[s, c, pl.ds(d * planes, planes)]
    lane = lax.broadcasted_iota(jnp.int32, (ny, nz), 1)
    row = jnp.zeros((ny, nz), jnp.float32)
    for s in range(snaps):
        row = jnp.where(lane == s, phase_ref[s], row)
    for d in range(n_dest):
        o_ref[d, rows - 1] = row


def packed_payload(frames, phases, n_dest):
    snaps, comps, nx, ny, nz = frames.shape
    rows = snaps * comps * (nx // n_dest) + 1
    return pl.pallas_call(
        pack_kernel,
        out_shape=jax.ShapeDtypeStruct((n_dest, rows, ny, nz), jnp.float32),
        in_specs=[pl.BlockSpec(memory_space=pltpu.SMEM), pl.BlockSpec(memory_space=pltpu.VMEM)],
        out_specs=pl.BlockSpec(memory_space=pltpu.VMEM),
        cost_estimate=pl.CostEstimate(
            flops=0, bytes_accessed=2 * frames.size * 4, transcendentals=0
        ),
    )(phases, frames)


def first_diff(shifted):
    return (
        0.75 * (shifted(1) - shifted(-1))
        - 0.15 * (shifted(2) - shifted(-2))
        + (shifted(3) - shifted(-3)) / 60.0
    )


def second_diff(shifted, centre):
    return (
        -49.0 / 18.0 * centre
        + 1.5 * (shifted(1) + shifted(-1))
        - 0.15 * (shifted(2) + shifted(-2))
        + (shifted(3) + shifted(-3)) / 90.0
    )


def ring(axis, step):
    count = lax.axis_size(axis)
    return [(i, (i + step) % count) for i in range(count)]


def stencil_kernel(f_ref, fl_ref, fr_ref, rp_ref, rn_ref, terms_ref, vel_ref):
    _, bins, planes, ny, nz = f_ref.shape

    def at(comp, b, x):
        if 0 <= x < planes:
            if 0 <= b < bins:
                return f_ref[comp, b, x]
            if b < 0:
                return rp_ref[comp - 3, b + HALO, x]
            return rn_ref[comp - 3, b - bins, x]
        if x < 0:
            return fl_ref[comp, b, x + planes]
        return fr_ref[comp, b, x - planes]

    def rolled(value, axis, size):
        table = {k: pltpu.roll(value, (-k) % size, axis) for k in (1, 2, 3, -1, -2, -3)}
        return lambda amount: table[amount]

    for b in range(bins):
        for x in range(planes):
            velocity = [f_ref[c, b, x] for c in range(3)]
            stresses = [f_ref[3 + m, b, x] for m in range(6)]
            for c in range(3):
                vel_ref[c, b, x] = velocity[c]
            grad_u = [
                [
                    first_diff(lambda k, c=c: at(c, b, x + k)),
                    first_diff(rolled(velocity[c], 0, ny)),
                    first_diff(rolled(velocity[c], 1, nz)),
                ]
                for c in range(3)
            ]
            for slot, (first, second) in enumerate(stress_pairs):
                comp = 3 + slot
                stress = stresses[slot]
                along_x = lambda k, comp=comp: at(comp, b, x + k)
                along_y = rolled(stress, 0, ny)
                along_z = rolled(stress, 1, nz)
                terms_ref[0, slot, b, x] = first_diff(lambda k, comp=comp: at(comp, b + k, x))
                grads = [first_diff(along_x), first_diff(along_y), first_diff(along_z)]
                terms_ref[1, slot, b, x] = (
                    velocity[0] * grads[0] + velocity[1] * grads[1] + velocity[2] * grads[2]
                )
                summed = jnp.zeros_like(stress)
                for dim in range(3):
                    summed = (
                        summed
                        + stresses[pair_index(first, dim)] * grad_u[second][dim]
                        + stresses[pair_index(second, dim)] * grad_u[first][dim]
                    )
                terms_ref[2, slot, b, x] = -summed
                terms_ref[3, slot, b, x] = viscosity * (
                    second_diff(along_x, stress)
                    + second_diff(along_y, stress)
                    + second_diff(along_z, stress)
                )


def finish_terms(fields, head, tail):
    _, bins_dev, planes, ny, nz = fields.shape
    from_left = lax.ppermute(fields, "rev", ring("rev", 1))
    from_right = lax.ppermute(fields, "rev", ring("rev", -1))
    from_prev = lax.ppermute(tail, "bin", ring("bin", 1))
    from_next = lax.ppermute(head, "bin", ring("bin", -1))
    cells = bins_dev * planes * ny * nz
    vmem = pl.BlockSpec(memory_space=pltpu.VMEM)
    return pl.pallas_call(
        stencil_kernel,
        out_shape=(
            jax.ShapeDtypeStruct((4, 6, bins_dev, planes, ny, nz), jnp.float32),
            jax.ShapeDtypeStruct((3, bins_dev, planes, ny, nz), jnp.float32),
        ),
        in_specs=[vmem] * 5,
        out_specs=(vmem, vmem),
        cost_estimate=pl.CostEstimate(
            flops=cells * 700,
            bytes_accessed=(3 * fields.size + 2 * head.size + 27 * cells) * 4,
            transcendentals=0,
        ),
    )(fields, from_left, from_right, from_prev, from_next)


def shards(snapshots, phase_index):
    bins_dev = PHASES // lax.axis_size("bin")
    n_rev = lax.axis_size("rev")
    frames = snapshots[0]
    snaps, comps, nx, ny, nz = frames.shape
    planes = nx // n_rev
    payload = packed_payload(frames, phase_index[0].astype(jnp.float32), n_rev)
    received = lax.all_to_all(payload, "rev", 0, 0, tiled=True)
    phases = received[:, -1, 0, :snaps].reshape(-1).astype(jnp.int32)
    local_bins = jnp.clip(phases - lax.axis_index("bin") * bins_dev, 0, bins_dev - 1)
    one_hot = local_bins[None, :] == jnp.arange(bins_dev, dtype=jnp.int32)[:, None]
    counts = jnp.sum(one_hot.astype(jnp.float32), axis=1)
    fields, head, tail = binned_fields(received, local_bins, counts, planes)
    return finish_terms(fields, head, tail)


def solution(mesh):
    in_specs = (P("rev", "bin", None, None, None, None), P("rev", "bin"))
    out_specs = (P(None, None, "bin", "rev", None, None), P(None, "bin", "rev", None, None))
    return jax.shard_map(shards, mesh=mesh, in_specs=in_specs, out_specs=out_specs, check_vma=False)
```

```python
import jax
import jax.numpy as jnp
from jax import lax
from jax.experimental import pallas as pl
from jax.experimental.pallas import tpu as pltpu
from jax.sharding import PartitionSpec as P

PHASES = 256
HALO = 3

viscosity = 0.2
stress_pairs = ((0, 0), (0, 1), (0, 2), (1, 1), (1, 2), (2, 2))


def pair_index(first, second):
    low, high = (min(first, second), max(first, second))
    return stress_pairs.index((low, high))


def bin_kernel(bins_ref, counts_ref, x_ref, o_ref, head_ref, tail_ref, acc_ref):
    bins, _, planes = acc_ref.shape[0], acc_ref.shape[1], acc_ref.shape[2]
    per_src = (x_ref.shape[1] - 1) // (3 * planes)
    snaps = x_ref.shape[0] * per_src
    acc_ref[...] = jnp.zeros(acc_ref.shape, jnp.float32)

    def body(s, carry):
        b = bins_ref[s]
        src = s // per_src
        base = (s % per_src) * (3 * planes)
        for p in range(planes):
            u = x_ref[src, base + p]
            v = x_ref[src, base + planes + p]
            w = x_ref[src, base + 2 * planes + p]
            moments = (u, v, w, u * u, u * v, u * w, v * v, v * w, w * w)
            for k in range(9):
                acc_ref[b, k, p] = acc_ref[b, k, p] + moments[k]
        return carry

    lax.fori_loop(0, snaps, body, 0)

    for b in range(bins):
        count = counts_ref[b]
        for p in range(planes):
            vel = [acc_ref[b, c, p] / count for c in range(3)]
            for c in range(3):
                o_ref[c, b, p] = vel[c]
            for slot, (i, j) in enumerate(stress_pairs):
                stress = acc_ref[b, 3 + slot, p] / count - vel[i] * vel[j]
                o_ref[3 + slot, b, p] = stress
                if b < HALO:
                    head_ref[slot, b, p] = stress
                if b >= bins - HALO:
                    tail_ref[slot, b - (bins - HALO), p] = stress


def binned_fields(received, local_bins, counts, planes):
    n_src, rows, ny, nz = received.shape
    bins = counts.shape[0]
    snaps = local_bins.shape[0]
    return pl.pallas_call(
        bin_kernel,
        out_shape=(
            jax.ShapeDtypeStruct((9, bins, planes, ny, nz), jnp.float32),
            jax.ShapeDtypeStruct((6, HALO, planes, ny, nz), jnp.float32),
            jax.ShapeDtypeStruct((6, HALO, planes, ny, nz), jnp.float32),
        ),
        in_specs=[
            pl.BlockSpec(memory_space=pltpu.SMEM),
            pl.BlockSpec(memory_space=pltpu.SMEM),
            pl.BlockSpec(memory_space=pltpu.VMEM),
        ],
        out_specs=(
            pl.BlockSpec(memory_space=pltpu.VMEM),
            pl.BlockSpec(memory_space=pltpu.VMEM),
            pl.BlockSpec(memory_space=pltpu.VMEM),
        ),
        scratch_shapes=[pltpu.VMEM((bins, 9, planes, ny, nz), jnp.float32)],
        cost_estimate=pl.CostEstimate(
            flops=snaps * planes * ny * nz * 15,
            bytes_accessed=received.size * 4 + 9 * bins * planes * ny * nz * 4,
            transcendentals=0,
        ),
    )(local_bins, counts, received)


def first_diff(shifted):
    return (
        0.75 * (shifted(1) - shifted(-1))
        - 0.15 * (shifted(2) - shifted(-2))
        + (shifted(3) - shifted(-3)) / 60.0
    )


def second_diff(shifted, centre):
    return (
        -49.0 / 18.0 * centre
        + 1.5 * (shifted(1) + shifted(-1))
        - 0.15 * (shifted(2) + shifted(-2))
        + (shifted(3) + shifted(-3)) / 90.0
    )


def ring(axis, step):
    count = lax.axis_size(axis)
    return [(i, (i + step) % count) for i in range(count)]


def halo_free_kernel(f_ref, part_ref):
    _, bins, planes, ny, nz = f_ref.shape

    def rolled(value, axis, size):
        table = {k: pltpu.roll(value, (-k) % size, axis) for k in (1, 2, 3, -1, -2, -3)}
        return lambda amount: table[amount]

    for b in range(bins):
        for x in range(planes):
            velocity = [f_ref[c, b, x] for c in range(3)]
            stresses = [f_ref[3 + m, b, x] for m in range(6)]
            grad_u = [
                [None, first_diff(rolled(velocity[c], 0, ny)), first_diff(rolled(velocity[c], 1, nz))]
                for c in range(3)
            ]
            for slot, (first, second) in enumerate(stress_pairs):
                stress = stresses[slot]
                along_y = rolled(stress, 0, ny)
                along_z = rolled(stress, 1, nz)
                part_ref[0, slot, b, x] = velocity[1] * first_diff(along_y) + velocity[2] * first_diff(along_z)
                summed = None
                for dim in (1, 2):
                    pair_sum = (
                        stresses[pair_index(first, dim)] * grad_u[second][dim]
                        + stresses[pair_index(second, dim)] * grad_u[first][dim]
                    )
                    summed = pair_sum if summed is None else summed + pair_sum
                part_ref[1, slot, b, x] = summed
                part_ref[2, slot, b, x] = second_diff(along_y, stress) + second_diff(along_z, stress)


def halo_kernel(f_ref, fl_ref, fr_ref, rp_ref, rn_ref, part_ref, terms_ref, vel_ref):
    _, bins, planes, ny, nz = f_ref.shape

    def at(comp, b, x):
        if 0 <= x < planes:
            if 0 <= b < bins:
                return f_ref[comp, b, x]
            if b < 0:
                return rp_ref[comp - 3, b + HALO, x]
            return rn_ref[comp - 3, b - bins, x]
        if x < 0:
            return fl_ref[comp, b, x + planes]
        return fr_ref[comp, b, x - planes]

    for b in range(bins):
        for x in range(planes):
            velocity = [f_ref[c, b, x] for c in range(3)]
            stresses = [f_ref[3 + m, b, x] for m in range(6)]
            for c in range(3):
                vel_ref[c, b, x] = velocity[c]
            grad_x = [first_diff(lambda k, c=c: at(c, b, x + k)) for c in range(3)]
            for slot, (first, second) in enumerate(stress_pairs):
                comp = 3 + slot
                stress = stresses[slot]
                along_x = lambda k, comp=comp: at(comp, b, x + k)
                terms_ref[0, slot, b, x] = first_diff(lambda k, comp=comp: at(comp, b + k, x))
                terms_ref[1, slot, b, x] = velocity[0] * first_diff(along_x) + part_ref[0, slot, b, x]
                terms_ref[2, slot, b, x] = -(
                    stresses[pair_index(first, 0)] * grad_x[second]
                    + stresses[pair_index(second, 0)] * grad_x[first]
                    + part_ref[1, slot, b, x]
                )
                terms_ref[3, slot, b, x] = viscosity * (
                    second_diff(along_x, stress) + part_ref[2, slot, b, x]
                )


def finish_terms(fields, head, tail):
    _, bins_dev, planes, ny, nz = fields.shape
    from_left = lax.ppermute(fields, "rev", ring("rev", 1))
    from_right = lax.ppermute(fields, "rev", ring("rev", -1))
    from_prev = lax.ppermute(tail, "bin", ring("bin", 1))
    from_next = lax.ppermute(head, "bin", ring("bin", -1))
    cells = bins_dev * planes * ny * nz
    vmem = pl.BlockSpec(memory_space=pltpu.VMEM)
    part = pl.pallas_call(
        halo_free_kernel,
        out_shape=jax.ShapeDtypeStruct((3, 6, bins_dev, planes, ny, nz), jnp.float32),
        in_specs=[vmem],
        out_specs=vmem,
        cost_estimate=pl.CostEstimate(
            flops=cells * 400, bytes_accessed=(9 + 18) * cells * 4, transcendentals=0
        ),
    )(fields)
    return pl.pallas_call(
        halo_kernel,
        out_shape=(
            jax.ShapeDtypeStruct((4, 6, bins_dev, planes, ny, nz), jnp.float32),
            jax.ShapeDtypeStruct((3, bins_dev, planes, ny, nz), jnp.float32),
        ),
        in_specs=[vmem] * 6,
        out_specs=(vmem, vmem),
        cost_estimate=pl.CostEstimate(
            flops=cells * 300,
            bytes_accessed=(3 * fields.size + 2 * head.size + 45 * cells) * 4,
            transcendentals=0,
        ),
    )(fields, from_left, from_right, from_prev, from_next, part)


def shards(snapshots, phase_index):
    bins_dev = PHASES // lax.axis_size("bin")
    n_rev = lax.axis_size("rev")
    frames = snapshots[0]
    snaps, comps, nx, ny, nz = frames.shape
    planes = nx // n_rev
    by_dest = frames.reshape(snaps, comps, n_rev, planes, ny, nz)
    by_dest = jnp.transpose(by_dest, (2, 0, 1, 3, 4, 5)).reshape(n_rev, snaps * comps * planes, ny, nz)
    phase_row = jnp.pad(phase_index[0].astype(jnp.float32), (0, nz - snaps))
    phase_slab = jnp.broadcast_to(phase_row[None, None, None, :], (n_rev, 1, ny, nz))
    payload = jnp.concatenate([by_dest, phase_slab], axis=1)
    received = lax.all_to_all(payload, "rev", 0, 0, tiled=True)
    phases = received[:, -1, 0, :snaps].reshape(-1).astype(jnp.int32)
    local_bins = jnp.clip(phases - lax.axis_index("bin") * bins_dev, 0, bins_dev - 1)
    one_hot = local_bins[None, :] == jnp.arange(bins_dev, dtype=jnp.int32)[:, None]
    counts = jnp.sum(one_hot.astype(jnp.float32), axis=1)
    fields, head, tail = binned_fields(received, local_bins, counts, planes)
    return finish_terms(fields, head, tail)


def solution(mesh):
    in_specs = (P("rev", "bin", None, None, None, None), P("rev", "bin"))
    out_specs = (P(None, None, "bin", "rev", None, None), P(None, "bin", "rev", None, None))
    return jax.shard_map(shards, mesh=mesh, in_specs=in_specs, out_specs=out_specs, check_vma=False)
```

```python
import jax
import jax.numpy as jnp
from jax import lax
from jax.experimental import pallas as pl
from jax.experimental.pallas import tpu as pltpu
from jax.sharding import PartitionSpec as P

PHASES = 256
HALO = 3

viscosity = 0.2
stress_pairs = ((0, 0), (0, 1), (0, 2), (1, 1), (1, 2), (2, 2))


def pair_index(first, second):
    low, high = (min(first, second), max(first, second))
    return stress_pairs.index((low, high))


def bin_kernel(bins_ref, x_ref, o_ref, head_ref, tail_ref, acc_ref):
    bins, _, planes = acc_ref.shape[0], acc_ref.shape[1], acc_ref.shape[2]
    per_src = (x_ref.shape[1] - 1) // (3 * planes)
    snaps = x_ref.shape[0] * per_src
    acc_ref[...] = jnp.zeros(acc_ref.shape, jnp.float32)

    def body(s, carry):
        b = bins_ref[s]
        src = s // per_src
        base = (s % per_src) * (3 * planes)
        for p in range(planes):
            u = x_ref[src, base + p]
            v = x_ref[src, base + planes + p]
            w = x_ref[src, base + 2 * planes + p]
            moments = (u, v, w, u * u, u * v, u * w, v * v, v * w, w * w)
            for k in range(9):
                acc_ref[b, k, p] = acc_ref[b, k, p] + moments[k]
        acc_ref[b, 9, 0] = acc_ref[b, 9, 0] + 1.0
        return carry

    lax.fori_loop(0, snaps, body, 0)

    for b in range(bins):
        count = acc_ref[b, 9, 0]
        for p in range(planes):
            vel = [acc_ref[b, c, p] / count for c in range(3)]
            for c in range(3):
                o_ref[c, b, p] = vel[c]
            for slot, (i, j) in enumerate(stress_pairs):
                stress = acc_ref[b, 3 + slot, p] / count - vel[i] * vel[j]
                o_ref[3 + slot, b, p] = stress
                if b < HALO:
                    head_ref[slot, b, p] = stress
                if b >= bins - HALO:
                    tail_ref[slot, b - (bins - HALO), p] = stress


def binned_fields(received, local_bins, bins, planes):
    n_src, rows, ny, nz = received.shape
    snaps = local_bins.shape[0]
    return pl.pallas_call(
        bin_kernel,
        out_shape=(
            jax.ShapeDtypeStruct((9, bins, planes, ny, nz), jnp.float32),
            jax.ShapeDtypeStruct((6, HALO, planes, ny, nz), jnp.float32),
            jax.ShapeDtypeStruct((6, HALO, planes, ny, nz), jnp.float32),
        ),
        in_specs=[pl.BlockSpec(memory_space=pltpu.SMEM), pl.BlockSpec(memory_space=pltpu.VMEM)],
        out_specs=(
            pl.BlockSpec(memory_space=pltpu.VMEM),
            pl.BlockSpec(memory_space=pltpu.VMEM),
            pl.BlockSpec(memory_space=pltpu.VMEM),
        ),
        scratch_shapes=[pltpu.VMEM((bins, 10, planes, ny, nz), jnp.float32)],
        cost_estimate=pl.CostEstimate(
            flops=snaps * planes * ny * nz * 15,
            bytes_accessed=received.size * 4 + 9 * bins * planes * ny * nz * 4,
            transcendentals=0,
        ),
    )(local_bins, received)


def first_diff(shifted):
    return (
        0.75 * (shifted(1) - shifted(-1))
        - 0.15 * (shifted(2) - shifted(-2))
        + (shifted(3) - shifted(-3)) / 60.0
    )


def second_diff(shifted, centre):
    return (
        -49.0 / 18.0 * centre
        + 1.5 * (shifted(1) + shifted(-1))
        - 0.15 * (shifted(2) + shifted(-2))
        + (shifted(3) + shifted(-3)) / 90.0
    )


def ring(axis, step):
    count = lax.axis_size(axis)
    return [(i, (i + step) % count) for i in range(count)]


def halo_free_kernel(f_ref, part_ref):
    _, bins, planes, ny, nz = f_ref.shape

    def rolled(value, axis, size):
        table = {k: pltpu.roll(value, (-k) % size, axis) for k in (1, 2, 3, -1, -2, -3)}
        return lambda amount: table[amount]

    for b in range(bins):
        for x in range(planes):
            velocity = [f_ref[c, b, x] for c in range(3)]
            stresses = [f_ref[3 + m, b, x] for m in range(6)]
            grad_u = [
                [None, first_diff(rolled(velocity[c], 0, ny)), first_diff(rolled(velocity[c], 1, nz))]
                for c in range(3)
            ]
            for slot, (first, second) in enumerate(stress_pairs):
                stress = stresses[slot]
                along_y = rolled(stress, 0, ny)
                along_z = rolled(stress, 1, nz)
                part_ref[0, slot, b, x] = velocity[1] * first_diff(along_y) + velocity[2] * first_diff(along_z)
                summed = None
                for dim in (1, 2):
                    pair_sum = (
                        stresses[pair_index(first, dim)] * grad_u[second][dim]
                        + stresses[pair_index(second, dim)] * grad_u[first][dim]
                    )
                    summed = pair_sum if summed is None else summed + pair_sum
                part_ref[1, slot, b, x] = summed
                part_ref[2, slot, b, x] = second_diff(along_y, stress) + second_diff(along_z, stress)


def halo_kernel(f_ref, fl_ref, fr_ref, rp_ref, rn_ref, part_ref, terms_ref, vel_ref):
    _, bins, planes, ny, nz = f_ref.shape

    def at(comp, b, x):
        if 0 <= x < planes:
            if 0 <= b < bins:
                return f_ref[comp, b, x]
            if b < 0:
                return rp_ref[comp - 3, b + HALO, x]
            return rn_ref[comp - 3, b - bins, x]
        if x < 0:
            return fl_ref[comp, b, x + planes]
        return fr_ref[comp, b, x - planes]

    for b in range(bins):
        for x in range(planes):
            velocity = [f_ref[c, b, x] for c in range(3)]
            stresses = [f_ref[3 + m, b, x] for m in range(6)]
            for c in range(3):
                vel_ref[c, b, x] = velocity[c]
            grad_x = [first_diff(lambda k, c=c: at(c, b, x + k)) for c in range(3)]
            for slot, (first, second) in enumerate(stress_pairs):
                comp = 3 + slot
                stress = stresses[slot]
                along_x = lambda k, comp=comp: at(comp, b, x + k)
                terms_ref[0, slot, b, x] = first_diff(lambda k, comp=comp: at(comp, b + k, x))
                terms_ref[1, slot, b, x] = velocity[0] * first_diff(along_x) + part_ref[0, slot, b, x]
                terms_ref[2, slot, b, x] = -(
                    stresses[pair_index(first, 0)] * grad_x[second]
                    + stresses[pair_index(second, 0)] * grad_x[first]
                    + part_ref[1, slot, b, x]
                )
                terms_ref[3, slot, b, x] = viscosity * (
                    second_diff(along_x, stress) + part_ref[2, slot, b, x]
                )


def finish_terms(fields, head, tail):
    _, bins_dev, planes, ny, nz = fields.shape
    from_left = lax.ppermute(fields, "rev", ring("rev", 1))
    from_right = lax.ppermute(fields, "rev", ring("rev", -1))
    from_prev = lax.ppermute(tail, "bin", ring("bin", 1))
    from_next = lax.ppermute(head, "bin", ring("bin", -1))
    cells = bins_dev * planes * ny * nz
    vmem = pl.BlockSpec(memory_space=pltpu.VMEM)
    part = pl.pallas_call(
        halo_free_kernel,
        out_shape=jax.ShapeDtypeStruct((3, 6, bins_dev, planes, ny, nz), jnp.float32),
        in_specs=[vmem],
        out_specs=vmem,
        cost_estimate=pl.CostEstimate(
            flops=cells * 400, bytes_accessed=(9 + 18) * cells * 4, transcendentals=0
        ),
    )(fields)
    return pl.pallas_call(
        halo_kernel,
        out_shape=(
            jax.ShapeDtypeStruct((4, 6, bins_dev, planes, ny, nz), jnp.float32),
            jax.ShapeDtypeStruct((3, bins_dev, planes, ny, nz), jnp.float32),
        ),
        in_specs=[vmem] * 6,
        out_specs=(vmem, vmem),
        cost_estimate=pl.CostEstimate(
            flops=cells * 300,
            bytes_accessed=(3 * fields.size + 2 * head.size + 45 * cells) * 4,
            transcendentals=0,
        ),
    )(fields, from_left, from_right, from_prev, from_next, part)


def shards(snapshots, phase_index):
    bins_dev = PHASES // lax.axis_size("bin")
    n_rev = lax.axis_size("rev")
    frames = snapshots[0]
    snaps, comps, nx, ny, nz = frames.shape
    planes = nx // n_rev
    by_dest = frames.reshape(snaps, comps, n_rev, planes, ny, nz)
    by_dest = jnp.transpose(by_dest, (2, 0, 1, 3, 4, 5)).reshape(n_rev, snaps * comps * planes, ny, nz)
    phase_row = jnp.pad(phase_index[0].astype(jnp.float32), (0, nz - snaps))
    phase_slab = jnp.broadcast_to(phase_row[None, None, None, :], (n_rev, 1, ny, nz))
    payload = jnp.concatenate([by_dest, phase_slab], axis=1)
    received = lax.all_to_all(payload, "rev", 0, 0, tiled=True)
    phases = received[:, -1, 0, :snaps].reshape(-1).astype(jnp.int32)
    local_bins = jnp.clip(phases - lax.axis_index("bin") * bins_dev, 0, bins_dev - 1)
    fields, head, tail = binned_fields(received, local_bins, bins_dev, planes)
    return finish_terms(fields, head, tail)


def solution(mesh):
    in_specs = (P("rev", "bin", None, None, None, None), P("rev", "bin"))
    out_specs = (P(None, None, "bin", "rev", None, None), P(None, "bin", "rev", None, None))
    return jax.shard_map(shards, mesh=mesh, in_specs=in_specs, out_specs=out_specs, check_vma=False)
```

```python
import jax
import jax.numpy as jnp
from jax import lax
from jax.experimental import pallas as pl
from jax.experimental.pallas import tpu as pltpu
from jax.sharding import PartitionSpec as P


PHASES = 256
HALO = 3

viscosity = 0.2
stress_pairs = ((0, 0), (0, 1), (0, 2), (1, 1), (1, 2), (2, 2))


def pair_index(first, second):
    low, high = (min(first, second), max(first, second))
    return stress_pairs.index((low, high))


def bin_kernel(bins_ref, x_ref, o_ref, head_ref, tail_ref, acc_ref):
    bins, planes = acc_ref.shape[0], acc_ref.shape[2]
    per_src = (x_ref.shape[1] - 1) // (3 * planes)
    snaps = x_ref.shape[0] * per_src
    acc_ref[...] = jnp.zeros(acc_ref.shape, jnp.float32)

    def body(s, carry):
        b = bins_ref[s]
        src = s // per_src
        base = (s % per_src) * (3 * planes)
        for p in range(planes):
            u = x_ref[src, base + p]
            v = x_ref[src, base + planes + p]
            w = x_ref[src, base + 2 * planes + p]
            moments = (u, v, w, u * u, u * v, u * w, v * v, v * w, w * w)
            for k in range(9):
                acc_ref[b, k, p] = acc_ref[b, k, p] + moments[k]
        acc_ref[b, 9, 0] = acc_ref[b, 9, 0] + 1.0
        return carry

    lax.fori_loop(0, snaps, body, 0)

    for b in range(bins):
        count = acc_ref[b, 9, 0]
        for p in range(planes):
            vel = [acc_ref[b, c, p] / count for c in range(3)]
            for c in range(3):
                o_ref[c, b, p] = vel[c]
            for slot, (i, j) in enumerate(stress_pairs):
                stress = acc_ref[b, 3 + slot, p] / count - vel[i] * vel[j]
                o_ref[3 + slot, b, p] = stress
                if b < HALO:
                    head_ref[slot, b, p] = stress
                if b >= bins - HALO:
                    tail_ref[slot, b - (bins - HALO), p] = stress


def binned_fields(received, local_bins, bins, planes):
    _, _, ny, nz = received.shape
    snaps = local_bins.shape[0]
    return pl.pallas_call(
        bin_kernel,
        out_shape=(
            jax.ShapeDtypeStruct((9, bins, planes, ny, nz), jnp.float32),
            jax.ShapeDtypeStruct((6, HALO, planes, ny, nz), jnp.float32),
            jax.ShapeDtypeStruct((6, HALO, planes, ny, nz), jnp.float32),
        ),
        in_specs=[pl.BlockSpec(memory_space=pltpu.SMEM), pl.BlockSpec(memory_space=pltpu.VMEM)],
        out_specs=(
            pl.BlockSpec(memory_space=pltpu.VMEM),
            pl.BlockSpec(memory_space=pltpu.VMEM),
            pl.BlockSpec(memory_space=pltpu.VMEM),
        ),
        scratch_shapes=[pltpu.VMEM((bins, 10, planes, ny, nz), jnp.float32)],
        cost_estimate=pl.CostEstimate(
            flops=snaps * planes * ny * nz * 15,
            bytes_accessed=received.size * 4 + 9 * bins * planes * ny * nz * 4,
            transcendentals=0,
        ),
    )(local_bins, received)


def first_diff(shifted):
    return (
        0.75 * (shifted(1) - shifted(-1))
        - 0.15 * (shifted(2) - shifted(-2))
        + (shifted(3) - shifted(-3)) / 60.0
    )


def second_diff(shifted, centre):
    return (
        -49.0 / 18.0 * centre
        + 1.5 * (shifted(1) + shifted(-1))
        - 0.15 * (shifted(2) + shifted(-2))
        + (shifted(3) + shifted(-3)) / 90.0
    )


def ring(axis, step):
    count = lax.axis_size(axis)
    return [(i, (i + step) % count) for i in range(count)]


def halo_free_kernel(f_ref, part_ref):
    _, bins, planes, ny, nz = f_ref.shape

    def rolled(value, axis, size):
        table = {k: pltpu.roll(value, (-k) % size, axis) for k in (1, 2, 3, -1, -2, -3)}
        return lambda amount: table[amount]

    for b in range(bins):
        for x in range(planes):
            velocity = [f_ref[c, b, x] for c in range(3)]
            stresses = [f_ref[3 + m, b, x] for m in range(6)]
            grad_u = [
                [None, first_diff(rolled(velocity[c], 0, ny)), first_diff(rolled(velocity[c], 1, nz))]
                for c in range(3)
            ]
            for slot, (first, second) in enumerate(stress_pairs):
                stress = stresses[slot]
                along_y = rolled(stress, 0, ny)
                along_z = rolled(stress, 1, nz)
                part_ref[0, slot, b, x] = velocity[1] * first_diff(along_y) + velocity[2] * first_diff(along_z)
                summed = None
                for dim in (1, 2):
                    pair_sum = (
                        stresses[pair_index(first, dim)] * grad_u[second][dim]
                        + stresses[pair_index(second, dim)] * grad_u[first][dim]
                    )
                    summed = pair_sum if summed is None else summed + pair_sum
                part_ref[1, slot, b, x] = summed
                part_ref[2, slot, b, x] = second_diff(along_y, stress) + second_diff(along_z, stress)


def halo_kernel(f_ref, fl_ref, fr_ref, rp_ref, rn_ref, part_ref, terms_ref, vel_ref):
    _, bins, planes, _, _ = f_ref.shape

    def at(comp, b, x):
        if 0 <= x < planes:
            if 0 <= b < bins:
                return f_ref[comp, b, x]
            if b < 0:
                return rp_ref[comp - 3, b + HALO, x]
            return rn_ref[comp - 3, b - bins, x]
        if x < 0:
            return fl_ref[comp, b, x + planes]
        return fr_ref[comp, b, x - planes]

    for b in range(bins):
        for x in range(planes):
            velocity = [f_ref[c, b, x] for c in range(3)]
            stresses = [f_ref[3 + m, b, x] for m in range(6)]
            for c in range(3):
                vel_ref[c, b, x] = velocity[c]
            grad_x = [first_diff(lambda k, c=c: at(c, b, x + k)) for c in range(3)]
            for slot, (first, second) in enumerate(stress_pairs):
                comp = 3 + slot
                stress = stresses[slot]
                along_x = lambda k, comp=comp: at(comp, b, x + k)
                terms_ref[0, slot, b, x] = first_diff(lambda k, comp=comp: at(comp, b + k, x))
                terms_ref[1, slot, b, x] = velocity[0] * first_diff(along_x) + part_ref[0, slot, b, x]
                terms_ref[2, slot, b, x] = -(
                    stresses[pair_index(first, 0)] * grad_x[second]
                    + stresses[pair_index(second, 0)] * grad_x[first]
                    + part_ref[1, slot, b, x]
                )
                terms_ref[3, slot, b, x] = viscosity * (
                    second_diff(along_x, stress) + part_ref[2, slot, b, x]
                )


def finish_terms(fields, head, tail):
    _, bins_dev, planes, ny, nz = fields.shape
    from_prev = lax.ppermute(tail, "bin", ring("bin", 1))
    from_next = lax.ppermute(head, "bin", ring("bin", -1))
    from_left = lax.ppermute(fields, "rev", ring("rev", 1))
    from_right = lax.ppermute(fields, "rev", ring("rev", -1))
    cells = bins_dev * planes * ny * nz
    vmem = pl.BlockSpec(memory_space=pltpu.VMEM)
    part = pl.pallas_call(
        halo_free_kernel,
        out_shape=jax.ShapeDtypeStruct((3, 6, bins_dev, planes, ny, nz), jnp.float32),
        in_specs=[vmem],
        out_specs=vmem,
        cost_estimate=pl.CostEstimate(
            flops=cells * 400, bytes_accessed=(9 + 18) * cells * 4, transcendentals=0
        ),
    )(fields)
    return pl.pallas_call(
        halo_kernel,
        out_shape=(
            jax.ShapeDtypeStruct((4, 6, bins_dev, planes, ny, nz), jnp.float32),
            jax.ShapeDtypeStruct((3, bins_dev, planes, ny, nz), jnp.float32),
        ),
        in_specs=[vmem] * 6,
        out_specs=(vmem, vmem),
        cost_estimate=pl.CostEstimate(
            flops=cells * 300,
            bytes_accessed=(3 * fields.size + 2 * head.size + 45 * cells) * 4,
            transcendentals=0,
        ),
    )(fields, from_left, from_right, from_prev, from_next, part)


def shards(snapshots, phase_index):
    bins_dev = PHASES // lax.axis_size("bin")
    n_rev = lax.axis_size("rev")
    frames = snapshots[0]
    snaps, comps, nx, ny, nz = frames.shape
    planes = nx // n_rev
    by_dest = frames.reshape(snaps, comps, n_rev, planes, ny, nz)
    by_dest = jnp.transpose(by_dest, (2, 0, 1, 3, 4, 5)).reshape(n_rev, snaps * comps * planes, ny, nz)
    phase_row = jnp.pad(phase_index[0].astype(jnp.float32), (0, nz - snaps))
    phase_slab = jnp.broadcast_to(phase_row[None, None, None, :], (n_rev, 1, ny, nz))
    payload = jnp.concatenate([by_dest, phase_slab], axis=1)
    received = lax.all_to_all(payload, "rev", 0, 0, tiled=True)
    phases = received[:, -1, 0, :snaps].reshape(-1).astype(jnp.int32)
    local_bins = jnp.clip(phases - lax.axis_index("bin") * bins_dev, 0, bins_dev - 1)
    fields, head, tail = binned_fields(received, local_bins, bins_dev, planes)
    return finish_terms(fields, head, tail)


def solution(mesh):
    in_specs = (P("rev", "bin", None, None, None, None), P("rev", "bin"))
    out_specs = (P(None, None, "bin", "rev", None, None), P(None, "bin", "rev", None, None))
    return jax.shard_map(shards, mesh=mesh, in_specs=in_specs, out_specs=out_specs, check_vma=False)
```

```python
import jax
import jax.numpy as jnp
from jax import lax
from jax.experimental import pallas as pl
from jax.experimental.pallas import tpu as pltpu
from jax.sharding import PartitionSpec as P

PHASES = 256
HALO = 3

viscosity = 0.2
stress_pairs = ((0, 0), (0, 1), (0, 2), (1, 1), (1, 2), (2, 2))


def pair_index(first, second):
    low, high = (min(first, second), max(first, second))
    return stress_pairs.index((low, high))


def bin_kernel(bins_ref, x_ref, o_ref, head_ref, tail_ref, acc_ref):
    bins, _, planes = acc_ref.shape[0], acc_ref.shape[1], acc_ref.shape[2]
    per_src = (x_ref.shape[1] - 1) // (3 * planes)
    snaps = x_ref.shape[0] * per_src
    acc_ref[...] = jnp.zeros(acc_ref.shape, jnp.float32)

    def body(s, carry):
        b = bins_ref[s]
        src = s // per_src
        base = (s % per_src) * (3 * planes)
        for p in range(planes):
            u = x_ref[src, base + p]
            v = x_ref[src, base + planes + p]
            w = x_ref[src, base + 2 * planes + p]
            moments = (u, v, w, u * u, u * v, u * w, v * v, v * w, w * w)
            for k in range(9):
                acc_ref[b, k, p] = acc_ref[b, k, p] + moments[k]
        acc_ref[b, 9, 0] = acc_ref[b, 9, 0] + 1.0
        return carry

    lax.fori_loop(0, snaps, body, 0)

    for b in range(bins):
        count = acc_ref[b, 9, 0]
        for p in range(planes):
            vel = [acc_ref[b, c, p] / count for c in range(3)]
            for c in range(3):
                o_ref[c, b, p] = vel[c]
            for slot, (i, j) in enumerate(stress_pairs):
                stress = acc_ref[b, 3 + slot, p] / count - vel[i] * vel[j]
                o_ref[3 + slot, b, p] = stress
                if b < HALO:
                    head_ref[slot, b, p] = stress
                if b >= bins - HALO:
                    tail_ref[slot, b - (bins - HALO), p] = stress


def binned_fields(received, local_bins, bins, planes):
    n_src, rows, ny, nz = received.shape
    snaps = local_bins.shape[0]
    return pl.pallas_call(
        bin_kernel,
        out_shape=(
            jax.ShapeDtypeStruct((9, bins, planes, ny, nz), jnp.float32),
            jax.ShapeDtypeStruct((6, HALO, planes, ny, nz), jnp.float32),
            jax.ShapeDtypeStruct((6, HALO, planes, ny, nz), jnp.float32),
        ),
        in_specs=[pl.BlockSpec(memory_space=pltpu.SMEM), pl.BlockSpec(memory_space=pltpu.VMEM)],
        out_specs=(
            pl.BlockSpec(memory_space=pltpu.VMEM),
            pl.BlockSpec(memory_space=pltpu.VMEM),
            pl.BlockSpec(memory_space=pltpu.VMEM),
        ),
        scratch_shapes=[pltpu.VMEM((bins, 10, planes, ny, nz), jnp.float32)],
        cost_estimate=pl.CostEstimate(
            flops=snaps * planes * ny * nz * 15,
            bytes_accessed=received.size * 4 + 9 * bins * planes * ny * nz * 4,
            transcendentals=0,
        ),
    )(local_bins, received)


def first_diff(shifted):
    return (
        0.75 * (shifted(1) - shifted(-1))
        - 0.15 * (shifted(2) - shifted(-2))
        + (shifted(3) - shifted(-3)) / 60.0
    )


def second_diff(shifted, centre):
    return (
        -49.0 / 18.0 * centre
        + 1.5 * (shifted(1) + shifted(-1))
        - 0.15 * (shifted(2) + shifted(-2))
        + (shifted(3) + shifted(-3)) / 90.0
    )


def ring(axis, step):
    count = lax.axis_size(axis)
    return [(i, (i + step) % count) for i in range(count)]


def halo_free_kernel(f_ref, part_ref, vel_ref):
    _, bins, planes, ny, nz = f_ref.shape

    def rolled(value, axis, size):
        table = {k: pltpu.roll(value, (-k) % size, axis) for k in (1, 2, 3, -1, -2, -3)}
        return lambda amount: table[amount]

    for b in range(bins):
        for x in range(planes):
            velocity = [f_ref[c, b, x] for c in range(3)]
            stresses = [f_ref[3 + m, b, x] for m in range(6)]
            for c in range(3):
                vel_ref[c, b, x] = velocity[c]
            grad_u = [
                [None, first_diff(rolled(velocity[c], 0, ny)), first_diff(rolled(velocity[c], 1, nz))]
                for c in range(3)
            ]
            for slot, (first, second) in enumerate(stress_pairs):
                stress = stresses[slot]
                along_y = rolled(stress, 0, ny)
                along_z = rolled(stress, 1, nz)
                part_ref[0, slot, b, x] = velocity[1] * first_diff(along_y) + velocity[2] * first_diff(along_z)
                summed = None
                for dim in (1, 2):
                    pair_sum = (
                        stresses[pair_index(first, dim)] * grad_u[second][dim]
                        + stresses[pair_index(second, dim)] * grad_u[first][dim]
                    )
                    summed = pair_sum if summed is None else summed + pair_sum
                part_ref[1, slot, b, x] = summed
                part_ref[2, slot, b, x] = second_diff(along_y, stress) + second_diff(along_z, stress)


def halo_kernel(f_ref, fl_ref, fr_ref, rp_ref, rn_ref, part_ref, terms_ref, ext_ref):
    _, bins, planes, ny, nz = f_ref.shape
    b = pl.program_id(0)

    @pl.when(b == 0)
    def _():
        for m in range(6):
            for j in range(HALO):
                ext_ref[m, j] = rp_ref[m, j]
                ext_ref[m, HALO + bins + j] = rn_ref[m, j]
            for j in range(bins):
                ext_ref[m, HALO + j] = f_ref[3 + m, j]

    def at(comp, x):
        if 0 <= x < planes:
            return f_ref[comp, b, x]
        if x < 0:
            return fl_ref[comp, 0, x + planes]
        return fr_ref[comp, 0, x - planes]

    for x in range(planes):
        velocity = [f_ref[c, b, x] for c in range(3)]
        stresses = [f_ref[3 + m, b, x] for m in range(6)]
        grad_x = [first_diff(lambda k, c=c: at(c, x + k)) for c in range(3)]
        for slot, (first, second) in enumerate(stress_pairs):
            comp = 3 + slot
            stress = stresses[slot]
            along_x = lambda k, comp=comp: at(comp, x + k)
            terms_ref[0, slot, 0, x] = first_diff(lambda k, slot=slot: ext_ref[slot, b + HALO + k, x])
            terms_ref[1, slot, 0, x] = velocity[0] * first_diff(along_x) + part_ref[0, slot, 0, x]
            terms_ref[2, slot, 0, x] = -(
                stresses[pair_index(first, 0)] * grad_x[second]
                + stresses[pair_index(second, 0)] * grad_x[first]
                + part_ref[1, slot, 0, x]
            )
            terms_ref[3, slot, 0, x] = viscosity * (second_diff(along_x, stress) + part_ref[2, slot, 0, x])


def finish_terms(fields, head, tail):
    _, bins_dev, planes, ny, nz = fields.shape
    from_left = lax.ppermute(fields, "rev", ring("rev", 1))
    from_right = lax.ppermute(fields, "rev", ring("rev", -1))
    from_prev = lax.ppermute(tail, "bin", ring("bin", 1))
    from_next = lax.ppermute(head, "bin", ring("bin", -1))
    cells = bins_dev * planes * ny * nz
    vmem = pl.BlockSpec(memory_space=pltpu.VMEM)
    part, mean_velocity = pl.pallas_call(
        halo_free_kernel,
        out_shape=(
            jax.ShapeDtypeStruct((3, 6, bins_dev, planes, ny, nz), jnp.float32),
            jax.ShapeDtypeStruct((3, bins_dev, planes, ny, nz), jnp.float32),
        ),
        in_specs=[vmem],
        out_specs=(vmem, vmem),
        cost_estimate=pl.CostEstimate(
            flops=cells * 400, bytes_accessed=(9 + 21) * cells * 4, transcendentals=0
        ),
    )(fields)
    whole = lambda shape: pl.BlockSpec(shape, lambda b: (0,) * len(shape))
    one_bin = lambda shape, axis: pl.BlockSpec(
        shape, lambda b: tuple(b if i == axis else 0 for i in range(len(shape)))
    )
    terms = pl.pallas_call(
        halo_kernel,
        grid=(bins_dev,),
        out_shape=jax.ShapeDtypeStruct((4, 6, bins_dev, planes, ny, nz), jnp.float32),
        in_specs=[
            whole(fields.shape),
            one_bin((9, 1, planes, ny, nz), 1),
            one_bin((9, 1, planes, ny, nz), 1),
            whole(head.shape),
            whole(head.shape),
            one_bin((3, 6, 1, planes, ny, nz), 2),
        ],
        out_specs=one_bin((4, 6, 1, planes, ny, nz), 2),
        scratch_shapes=[pltpu.VMEM((6, bins_dev + 2 * HALO, planes, ny, nz), jnp.float32)],
        cost_estimate=pl.CostEstimate(
            flops=cells * 300,
            bytes_accessed=(3 * fields.size + 2 * head.size + 42 * cells) * 4,
            transcendentals=0,
        ),
    )(fields, from_left, from_right, from_prev, from_next, part)
    return terms, mean_velocity


def shards(snapshots, phase_index):
    bins_dev = PHASES // lax.axis_size("bin")
    n_rev = lax.axis_size("rev")
    frames = snapshots[0]
    snaps, comps, nx, ny, nz = frames.shape
    planes = nx // n_rev
    by_dest = frames.reshape(snaps, comps, n_rev, planes, ny, nz)
    by_dest = jnp.transpose(by_dest, (2, 0, 1, 3, 4, 5)).reshape(n_rev, snaps * comps * planes, ny, nz)
    phase_row = jnp.pad(phase_index[0].astype(jnp.float32), (0, nz - snaps))
    phase_slab = jnp.broadcast_to(phase_row[None, None, None, :], (n_rev, 1, ny, nz))
    payload = jnp.concatenate([by_dest, phase_slab], axis=1)
    received = lax.all_to_all(payload, "rev", 0, 0, tiled=True)
    phases = received[:, -1, 0, :snaps].reshape(-1).astype(jnp.int32)
    local_bins = jnp.clip(phases - lax.axis_index("bin") * bins_dev, 0, bins_dev - 1)
    fields, head, tail = binned_fields(received, local_bins, bins_dev, planes)
    return finish_terms(fields, head, tail)


def solution(mesh):
    in_specs = (P("rev", "bin", None, None, None, None), P("rev", "bin"))
    out_specs = (P(None, None, "bin", "rev", None, None), P(None, "bin", "rev", None, None))
    return jax.shard_map(shards, mesh=mesh, in_specs=in_specs, out_specs=out_specs, check_vma=False)
```

```python
import jax
import jax.numpy as jnp
from jax import lax
from jax.experimental import pallas as pl
from jax.experimental.pallas import tpu as pltpu
from jax.sharding import PartitionSpec as P

PHASES = 256
HALO = 3

viscosity = 0.2
stress_pairs = ((0, 0), (0, 1), (0, 2), (1, 1), (1, 2), (2, 2))


def pair_index(first, second):
    low, high = (min(first, second), max(first, second))
    return stress_pairs.index((low, high))


def bin_kernel(bins_ref, x_ref, o_ref, head_ref, tail_ref, acc_ref):
    bins, planes = acc_ref.shape[0], acc_ref.shape[2]
    per_src = (x_ref.shape[1] - 1) // (3 * planes)
    src = pl.program_id(0)

    @pl.when(src == 0)
    def _():
        acc_ref[...] = jnp.zeros(acc_ref.shape, jnp.float32)

    def body(j, carry):
        b = bins_ref[src * per_src + j]
        base = j * (3 * planes)
        for p in range(planes):
            u = x_ref[0, base + p]
            v = x_ref[0, base + planes + p]
            w = x_ref[0, base + 2 * planes + p]
            moments = (u, v, w, u * u, u * v, u * w, v * v, v * w, w * w)
            for k in range(9):
                acc_ref[b, k, p] = acc_ref[b, k, p] + moments[k]
        acc_ref[b, 9, 0] = acc_ref[b, 9, 0] + 1.0
        return carry

    lax.fori_loop(0, per_src, body, 0)

    @pl.when(src == pl.num_programs(0) - 1)
    def _():
        for b in range(bins):
            count = acc_ref[b, 9, 0]
            for p in range(planes):
                vel = [acc_ref[b, c, p] / count for c in range(3)]
                for c in range(3):
                    o_ref[c, b, p] = vel[c]
                for slot, (i, j) in enumerate(stress_pairs):
                    stress = acc_ref[b, 3 + slot, p] / count - vel[i] * vel[j]
                    o_ref[3 + slot, b, p] = stress
                    if b < HALO:
                        head_ref[slot, b, p] = stress
                    if b >= bins - HALO:
                        tail_ref[slot, b - (bins - HALO), p] = stress


def binned_fields(received, local_bins, bins, planes):
    n_src, rows, ny, nz = received.shape
    snaps = local_bins.shape[0]
    whole = lambda shape: pl.BlockSpec(shape, lambda i: (0,) * len(shape))
    return pl.pallas_call(
        bin_kernel,
        grid=(n_src,),
        out_shape=(
            jax.ShapeDtypeStruct((9, bins, planes, ny, nz), jnp.float32),
            jax.ShapeDtypeStruct((6, HALO, planes, ny, nz), jnp.float32),
            jax.ShapeDtypeStruct((6, HALO, planes, ny, nz), jnp.float32),
        ),
        in_specs=[
            pl.BlockSpec(memory_space=pltpu.SMEM),
            pl.BlockSpec((1, rows, ny, nz), lambda i: (i, 0, 0, 0)),
        ],
        out_specs=(
            whole((9, bins, planes, ny, nz)),
            whole((6, HALO, planes, ny, nz)),
            whole((6, HALO, planes, ny, nz)),
        ),
        scratch_shapes=[pltpu.VMEM((bins, 10, planes, ny, nz), jnp.float32)],
        cost_estimate=pl.CostEstimate(
            flops=snaps * planes * ny * nz * 15,
            bytes_accessed=received.size * 4 + 9 * bins * planes * ny * nz * 4,
            transcendentals=0,
        ),
    )(local_bins, received)


def first_diff(shifted):
    return (
        0.75 * (shifted(1) - shifted(-1))
        - 0.15 * (shifted(2) - shifted(-2))
        + (shifted(3) - shifted(-3)) / 60.0
    )


def second_diff(shifted, centre):
    return (
        -49.0 / 18.0 * centre
        + 1.5 * (shifted(1) + shifted(-1))
        - 0.15 * (shifted(2) + shifted(-2))
        + (shifted(3) + shifted(-3)) / 90.0
    )


def ring(axis, step):
    count = lax.axis_size(axis)
    return [(i, (i + step) % count) for i in range(count)]


def halo_free_kernel(f_ref, part_ref):
    _, bins, planes, ny, nz = f_ref.shape

    def rolled(value, axis, size):
        table = {k: pltpu.roll(value, (-k) % size, axis) for k in (1, 2, 3, -1, -2, -3)}
        return lambda amount: table[amount]

    for b in range(bins):
        for x in range(planes):
            velocity = [f_ref[c, b, x] for c in range(3)]
            stresses = [f_ref[3 + m, b, x] for m in range(6)]
            grad_u = [
                [None, first_diff(rolled(velocity[c], 0, ny)), first_diff(rolled(velocity[c], 1, nz))]
                for c in range(3)
            ]
            for slot, (first, second) in enumerate(stress_pairs):
                stress = stresses[slot]
                along_y = rolled(stress, 0, ny)
                along_z = rolled(stress, 1, nz)
                part_ref[0, slot, b, x] = velocity[1] * first_diff(along_y) + velocity[2] * first_diff(along_z)
                summed = None
                for dim in (1, 2):
                    pair_sum = (
                        stresses[pair_index(first, dim)] * grad_u[second][dim]
                        + stresses[pair_index(second, dim)] * grad_u[first][dim]
                    )
                    summed = pair_sum if summed is None else summed + pair_sum
                part_ref[1, slot, b, x] = summed
                part_ref[2, slot, b, x] = second_diff(along_y, stress) + second_diff(along_z, stress)


def halo_kernel(f_ref, fl_ref, fr_ref, rp_ref, rn_ref, part_ref, terms_ref, vel_ref):
    _, bins, planes, ny, nz = f_ref.shape

    def at(comp, b, x):
        if 0 <= x < planes:
            if 0 <= b < bins:
                return f_ref[comp, b, x]
            if b < 0:
                return rp_ref[comp - 3, b + HALO, x]
            return rn_ref[comp - 3, b - bins, x]
        if x < 0:
            return fl_ref[comp, b, x + planes]
        return fr_ref[comp, b, x - planes]

    for b in range(bins):
        for x in range(planes):
            velocity = [f_ref[c, b, x] for c in range(3)]
            stresses = [f_ref[3 + m, b, x] for m in range(6)]
            for c in range(3):
                vel_ref[c, b, x] = velocity[c]
            grad_x = [first_diff(lambda k, c=c: at(c, b, x + k)) for c in range(3)]
            for slot, (first, second) in enumerate(stress_pairs):
                comp = 3 + slot
                stress = stresses[slot]
                along_x = lambda k, comp=comp: at(comp, b, x + k)
                terms_ref[0, slot, b, x] = first_diff(lambda k, comp=comp: at(comp, b + k, x))
                terms_ref[1, slot, b, x] = velocity[0] * first_diff(along_x) + part_ref[0, slot, b, x]
                terms_ref[2, slot, b, x] = -(
                    stresses[pair_index(first, 0)] * grad_x[second]
                    + stresses[pair_index(second, 0)] * grad_x[first]
                    + part_ref[1, slot, b, x]
                )
                terms_ref[3, slot, b, x] = viscosity * (
                    second_diff(along_x, stress) + part_ref[2, slot, b, x]
                )


def finish_terms(fields, head, tail):
    _, bins_dev, planes, ny, nz = fields.shape
    from_left = lax.ppermute(fields, "rev", ring("rev", 1))
    from_right = lax.ppermute(fields, "rev", ring("rev", -1))
    from_prev = lax.ppermute(tail, "bin", ring("bin", 1))
    from_next = lax.ppermute(head, "bin", ring("bin", -1))
    cells = bins_dev * planes * ny * nz
    vmem = pl.BlockSpec(memory_space=pltpu.VMEM)
    part = pl.pallas_call(
        halo_free_kernel,
        out_shape=jax.ShapeDtypeStruct((3, 6, bins_dev, planes, ny, nz), jnp.float32),
        in_specs=[vmem],
        out_specs=vmem,
        cost_estimate=pl.CostEstimate(
            flops=cells * 400, bytes_accessed=(9 + 18) * cells * 4, transcendentals=0
        ),
    )(fields)
    return pl.pallas_call(
        halo_kernel,
        out_shape=(
            jax.ShapeDtypeStruct((4, 6, bins_dev, planes, ny, nz), jnp.float32),
            jax.ShapeDtypeStruct((3, bins_dev, planes, ny, nz), jnp.float32),
        ),
        in_specs=[vmem] * 6,
        out_specs=(vmem, vmem),
        cost_estimate=pl.CostEstimate(
            flops=cells * 300,
            bytes_accessed=(3 * fields.size + 2 * head.size + 45 * cells) * 4,
            transcendentals=0,
        ),
    )(fields, from_left, from_right, from_prev, from_next, part)


def shards(snapshots, phase_index):
    bins_dev = PHASES // lax.axis_size("bin")
    n_rev = lax.axis_size("rev")
    frames = snapshots[0]
    snaps, comps, nx, ny, nz = frames.shape
    planes = nx // n_rev
    by_dest = frames.reshape(snaps, comps, n_rev, planes, ny, nz)
    by_dest = jnp.transpose(by_dest, (2, 0, 1, 3, 4, 5)).reshape(n_rev, snaps * comps * planes, ny, nz)
    phase_row = jnp.pad(phase_index[0].astype(jnp.float32), (0, nz - snaps))
    phase_slab = jnp.broadcast_to(phase_row[None, None, None, :], (n_rev, 1, ny, nz))
    payload = jnp.concatenate([by_dest, phase_slab], axis=1)
    received = lax.all_to_all(payload, "rev", 0, 0, tiled=True)
    phases = received[:, -1, 0, :snaps].reshape(-1).astype(jnp.int32)
    local_bins = jnp.clip(phases - lax.axis_index("bin") * bins_dev, 0, bins_dev - 1)
    fields, head, tail = binned_fields(received, local_bins, bins_dev, planes)
    return finish_terms(fields, head, tail)


def solution(mesh):
    in_specs = (P("rev", "bin", None, None, None, None), P("rev", "bin"))
    out_specs = (P(None, None, "bin", "rev", None, None), P(None, "bin", "rev", None, None))
    return jax.shard_map(shards, mesh=mesh, in_specs=in_specs, out_specs=out_specs, check_vma=False)
```

```python
import jax
import jax.numpy as jnp
from jax import lax
from jax.experimental import pallas as pl
from jax.experimental.pallas import tpu as pltpu
from jax.sharding import PartitionSpec as P

PHASES = 256
HALO = 3

viscosity = 0.2
stress_pairs = ((0, 0), (0, 1), (0, 2), (1, 1), (1, 2), (2, 2))


def pair_index(first, second):
    low, high = (min(first, second), max(first, second))
    return stress_pairs.index((low, high))


def bin_kernel(bins_ref, x_ref, o_ref, head_ref, tail_ref, acc_ref):
    bins, _, planes = acc_ref.shape[0], acc_ref.shape[1], acc_ref.shape[2]
    per_src = (x_ref.shape[1] - 1) // (3 * planes)
    snaps = x_ref.shape[0] * per_src
    acc_ref[...] = jnp.zeros(acc_ref.shape, jnp.float32)

    def body(s, carry):
        b = bins_ref[s]
        src = s // per_src
        base = (s % per_src) * (3 * planes)
        for p in range(planes):
            u = x_ref[src, base + p]
            v = x_ref[src, base + planes + p]
            w = x_ref[src, base + 2 * planes + p]
            moments = (u, v, w, u * u, u * v, u * w, v * v, v * w, w * w)
            for k in range(9):
                acc_ref[b, k, p] = acc_ref[b, k, p] + moments[k]
        acc_ref[b, 9, 0] = acc_ref[b, 9, 0] + 1.0
        return carry

    lax.fori_loop(0, snaps, body, 0, unroll=2)

    for b in range(bins):
        count = acc_ref[b, 9, 0]
        for p in range(planes):
            vel = [acc_ref[b, c, p] / count for c in range(3)]
            for c in range(3):
                o_ref[c, b, p] = vel[c]
            for slot, (i, j) in enumerate(stress_pairs):
                stress = acc_ref[b, 3 + slot, p] / count - vel[i] * vel[j]
                o_ref[3 + slot, b, p] = stress
                if b < HALO:
                    head_ref[slot, b, p] = stress
                if b >= bins - HALO:
                    tail_ref[slot, b - (bins - HALO), p] = stress


def binned_fields(received, local_bins, bins, planes):
    n_src, rows, ny, nz = received.shape
    snaps = local_bins.shape[0]
    return pl.pallas_call(
        bin_kernel,
        out_shape=(
            jax.ShapeDtypeStruct((9, bins, planes, ny, nz), jnp.float32),
            jax.ShapeDtypeStruct((6, HALO, planes, ny, nz), jnp.float32),
            jax.ShapeDtypeStruct((6, HALO, planes, ny, nz), jnp.float32),
        ),
        in_specs=[pl.BlockSpec(memory_space=pltpu.SMEM), pl.BlockSpec(memory_space=pltpu.VMEM)],
        out_specs=(
            pl.BlockSpec(memory_space=pltpu.VMEM),
            pl.BlockSpec(memory_space=pltpu.VMEM),
            pl.BlockSpec(memory_space=pltpu.VMEM),
        ),
        scratch_shapes=[pltpu.VMEM((bins, 10, planes, ny, nz), jnp.float32)],
        cost_estimate=pl.CostEstimate(
            flops=snaps * planes * ny * nz * 15,
            bytes_accessed=received.size * 4 + 9 * bins * planes * ny * nz * 4,
            transcendentals=0,
        ),
    )(local_bins, received)


def first_diff(shifted):
    return (
        0.75 * (shifted(1) - shifted(-1))
        - 0.15 * (shifted(2) - shifted(-2))
        + (shifted(3) - shifted(-3)) / 60.0
    )


def second_diff(shifted, centre):
    return (
        -49.0 / 18.0 * centre
        + 1.5 * (shifted(1) + shifted(-1))
        - 0.15 * (shifted(2) + shifted(-2))
        + (shifted(3) + shifted(-3)) / 90.0
    )


def ring(axis, step):
    count = lax.axis_size(axis)
    return [(i, (i + step) % count) for i in range(count)]


def halo_free_kernel(f_ref, part_ref):
    _, bins, planes, ny, nz = f_ref.shape

    def rolled(value, axis, size):
        table = {k: pltpu.roll(value, (-k) % size, axis) for k in (1, 2, 3, -1, -2, -3)}
        return lambda amount: table[amount]

    for b in range(bins):
        for x in range(planes):
            velocity = [f_ref[c, b, x] for c in range(3)]
            stresses = [f_ref[3 + m, b, x] for m in range(6)]
            grad_u = [
                [None, first_diff(rolled(velocity[c], 0, ny)), first_diff(rolled(velocity[c], 1, nz))]
                for c in range(3)
            ]
            for slot, (first, second) in enumerate(stress_pairs):
                stress = stresses[slot]
                along_y = rolled(stress, 0, ny)
                along_z = rolled(stress, 1, nz)
                part_ref[0, slot, b, x] = velocity[1] * first_diff(along_y) + velocity[2] * first_diff(along_z)
                summed = None
                for dim in (1, 2):
                    pair_sum = (
                        stresses[pair_index(first, dim)] * grad_u[second][dim]
                        + stresses[pair_index(second, dim)] * grad_u[first][dim]
                    )
                    summed = pair_sum if summed is None else summed + pair_sum
                part_ref[1, slot, b, x] = summed
                part_ref[2, slot, b, x] = second_diff(along_y, stress) + second_diff(along_z, stress)


def halo_kernel(f_ref, fl_ref, fr_ref, rp_ref, rn_ref, part_ref, terms_ref, vel_ref):
    _, bins, planes, ny, nz = f_ref.shape

    def at(comp, b, x):
        if 0 <= x < planes:
            if 0 <= b < bins:
                return f_ref[comp, b, x]
            if b < 0:
                return rp_ref[comp - 3, b + HALO, x]
            return rn_ref[comp - 3, b - bins, x]
        if x < 0:
            return fl_ref[comp, b, x + planes]
        return fr_ref[comp, b, x - planes]

    for b in range(bins):
        for x in range(planes):
            velocity = [f_ref[c, b, x] for c in range(3)]
            stresses = [f_ref[3 + m, b, x] for m in range(6)]
            for c in range(3):
                vel_ref[c, b, x] = velocity[c]
            grad_x = [first_diff(lambda k, c=c: at(c, b, x + k)) for c in range(3)]
            for slot, (first, second) in enumerate(stress_pairs):
                comp = 3 + slot
                stress = stresses[slot]
                along_x = lambda k, comp=comp: at(comp, b, x + k)
                terms_ref[0, slot, b, x] = first_diff(lambda k, comp=comp: at(comp, b + k, x))
                terms_ref[1, slot, b, x] = velocity[0] * first_diff(along_x) + part_ref[0, slot, b, x]
                terms_ref[2, slot, b, x] = -(
                    stresses[pair_index(first, 0)] * grad_x[second]
                    + stresses[pair_index(second, 0)] * grad_x[first]
                    + part_ref[1, slot, b, x]
                )
                terms_ref[3, slot, b, x] = viscosity * (
                    second_diff(along_x, stress) + part_ref[2, slot, b, x]
                )


def finish_terms(fields, head, tail):
    _, bins_dev, planes, ny, nz = fields.shape
    from_left = lax.ppermute(fields, "rev", ring("rev", 1))
    from_right = lax.ppermute(fields, "rev", ring("rev", -1))
    from_prev = lax.ppermute(tail, "bin", ring("bin", 1))
    from_next = lax.ppermute(head, "bin", ring("bin", -1))
    cells = bins_dev * planes * ny * nz
    vmem = pl.BlockSpec(memory_space=pltpu.VMEM)
    part = pl.pallas_call(
        halo_free_kernel,
        out_shape=jax.ShapeDtypeStruct((3, 6, bins_dev, planes, ny, nz), jnp.float32),
        in_specs=[vmem],
        out_specs=vmem,
        cost_estimate=pl.CostEstimate(
            flops=cells * 400, bytes_accessed=(9 + 18) * cells * 4, transcendentals=0
        ),
    )(fields)
    return pl.pallas_call(
        halo_kernel,
        out_shape=(
            jax.ShapeDtypeStruct((4, 6, bins_dev, planes, ny, nz), jnp.float32),
            jax.ShapeDtypeStruct((3, bins_dev, planes, ny, nz), jnp.float32),
        ),
        in_specs=[vmem] * 6,
        out_specs=(vmem, vmem),
        cost_estimate=pl.CostEstimate(
            flops=cells * 300,
            bytes_accessed=(3 * fields.size + 2 * head.size + 45 * cells) * 4,
            transcendentals=0,
        ),
    )(fields, from_left, from_right, from_prev, from_next, part)


def shards(snapshots, phase_index):
    bins_dev = PHASES // lax.axis_size("bin")
    n_rev = lax.axis_size("rev")
    frames = snapshots[0]
    snaps, comps, nx, ny, nz = frames.shape
    planes = nx // n_rev
    by_dest = frames.reshape(snaps, comps, n_rev, planes, ny, nz)
    by_dest = jnp.transpose(by_dest, (2, 0, 1, 3, 4, 5)).reshape(n_rev, snaps * comps * planes, ny, nz)
    phase_row = jnp.pad(phase_index[0].astype(jnp.float32), (0, nz - snaps))
    phase_slab = jnp.broadcast_to(phase_row[None, None, None, :], (n_rev, 1, ny, nz))
    payload = jnp.concatenate([by_dest, phase_slab], axis=1)
    received = lax.all_to_all(payload, "rev", 0, 0, tiled=True)
    phases = received[:, -1, 0, :snaps].reshape(-1).astype(jnp.int32)
    local_bins = jnp.clip(phases - lax.axis_index("bin") * bins_dev, 0, bins_dev - 1)
    fields, head, tail = binned_fields(received, local_bins, bins_dev, planes)
    return finish_terms(fields, head, tail)


def solution(mesh):
    in_specs = (P("rev", "bin", None, None, None, None), P("rev", "bin"))
    out_specs = (P(None, None, "bin", "rev", None, None), P(None, "bin", "rev", None, None))
    return jax.shard_map(shards, mesh=mesh, in_specs=in_specs, out_specs=out_specs, check_vma=False)
```

```python
import jax
import jax.numpy as jnp
from jax import lax
from jax.experimental import pallas as pl
from jax.experimental.pallas import tpu as pltpu
from jax.sharding import PartitionSpec as P

PHASES = 256
HALO = 3

viscosity = 0.2
stress_pairs = ((0, 0), (0, 1), (0, 2), (1, 1), (1, 2), (2, 2))


def pair_index(first, second):
    low, high = (min(first, second), max(first, second))
    return stress_pairs.index((low, high))


def bin_kernel(bins_ref, x_ref, o_ref, head_ref, tail_ref, acc_ref):
    bins, _, planes = acc_ref.shape[0], acc_ref.shape[1], acc_ref.shape[2]
    per_src = (x_ref.shape[1] - 1) // (3 * planes)
    snaps = x_ref.shape[0] * per_src
    acc_ref[...] = jnp.zeros(acc_ref.shape, jnp.float32)

    def body(s, carry):
        b = bins_ref[s]
        src = s // per_src
        base = (s % per_src) * (3 * planes)
        for p in range(planes):
            u = x_ref[src, base + p]
            v = x_ref[src, base + planes + p]
            w = x_ref[src, base + 2 * planes + p]
            moments = (u, v, w, u * u, u * v, u * w, v * v, v * w, w * w)
            for k in range(9):
                acc_ref[b, k, p] = acc_ref[b, k, p] + moments[k]
        acc_ref[b, 9, 0] = acc_ref[b, 9, 0] + 1.0
        return carry

    lax.fori_loop(0, snaps, body, 0, unroll=2)

    for b in range(bins):
        count = acc_ref[b, 9, 0]
        for p in range(planes):
            vel = [acc_ref[b, c, p] / count for c in range(3)]
            for c in range(3):
                o_ref[c, b, p] = vel[c]
            for slot, (i, j) in enumerate(stress_pairs):
                stress = acc_ref[b, 3 + slot, p] / count - vel[i] * vel[j]
                o_ref[3 + slot, b, p] = stress
                if b < HALO:
                    head_ref[slot, b, p] = stress
                if b >= bins - HALO:
                    tail_ref[slot, b - (bins - HALO), p] = stress


def binned_fields(received, local_bins, bins, planes):
    n_src, rows, ny, nz = received.shape
    snaps = local_bins.shape[0]
    return pl.pallas_call(
        bin_kernel,
        out_shape=(
            jax.ShapeDtypeStruct((9, bins, planes, ny, nz), jnp.float32),
            jax.ShapeDtypeStruct((6, HALO, planes, ny, nz), jnp.float32),
            jax.ShapeDtypeStruct((6, HALO, planes, ny, nz), jnp.float32),
        ),
        in_specs=[pl.BlockSpec(memory_space=pltpu.SMEM), pl.BlockSpec(memory_space=pltpu.VMEM)],
        out_specs=(
            pl.BlockSpec(memory_space=pltpu.VMEM),
            pl.BlockSpec(memory_space=pltpu.VMEM),
            pl.BlockSpec(memory_space=pltpu.VMEM),
        ),
        scratch_shapes=[pltpu.VMEM((bins, 10, planes, ny, nz), jnp.float32)],
        compiler_params=pltpu.CompilerParams(vmem_limit_bytes=16 * 1024 * 1024),
        cost_estimate=pl.CostEstimate(
            flops=snaps * planes * ny * nz * 15,
            bytes_accessed=received.size * 4 + 9 * bins * planes * ny * nz * 4,
            transcendentals=0,
        ),
    )(local_bins, received)


def first_diff(shifted):
    return (
        0.75 * (shifted(1) - shifted(-1))
        - 0.15 * (shifted(2) - shifted(-2))
        + (shifted(3) - shifted(-3)) / 60.0
    )


def second_diff(shifted, centre):
    return (
        -49.0 / 18.0 * centre
        + 1.5 * (shifted(1) + shifted(-1))
        - 0.15 * (shifted(2) + shifted(-2))
        + (shifted(3) + shifted(-3)) / 90.0
    )


def ring(axis, step):
    count = lax.axis_size(axis)
    return [(i, (i + step) % count) for i in range(count)]


def halo_free_kernel(f_ref, part_ref):
    _, bins, planes, ny, nz = f_ref.shape

    def rolled(value, axis, size):
        table = {k: pltpu.roll(value, (-k) % size, axis) for k in (1, 2, 3, -1, -2, -3)}
        return lambda amount: table[amount]

    for b in range(bins):
        for x in range(planes):
            velocity = [f_ref[c, b, x] for c in range(3)]
            stresses = [f_ref[3 + m, b, x] for m in range(6)]
            grad_u = [
                [None, first_diff(rolled(velocity[c], 0, ny)), first_diff(rolled(velocity[c], 1, nz))]
                for c in range(3)
            ]
            for slot, (first, second) in enumerate(stress_pairs):
                stress = stresses[slot]
                along_y = rolled(stress, 0, ny)
                along_z = rolled(stress, 1, nz)
                part_ref[0, slot, b, x] = velocity[1] * first_diff(along_y) + velocity[2] * first_diff(along_z)
                summed = None
                for dim in (1, 2):
                    pair_sum = (
                        stresses[pair_index(first, dim)] * grad_u[second][dim]
                        + stresses[pair_index(second, dim)] * grad_u[first][dim]
                    )
                    summed = pair_sum if summed is None else summed + pair_sum
                part_ref[1, slot, b, x] = summed
                part_ref[2, slot, b, x] = second_diff(along_y, stress) + second_diff(along_z, stress)


def halo_kernel(f_ref, fl_ref, fr_ref, rp_ref, rn_ref, part_ref, terms_ref, vel_ref):
    _, bins, planes, ny, nz = f_ref.shape

    def at(comp, b, x):
        if 0 <= x < planes:
            if 0 <= b < bins:
                return f_ref[comp, b, x]
            if b < 0:
                return rp_ref[comp - 3, b + HALO, x]
            return rn_ref[comp - 3, b - bins, x]
        if x < 0:
            return fl_ref[comp, b, x + planes]
        return fr_ref[comp, b, x - planes]

    for b in range(bins):
        for x in range(planes):
            velocity = [f_ref[c, b, x] for c in range(3)]
            stresses = [f_ref[3 + m, b, x] for m in range(6)]
            for c in range(3):
                vel_ref[c, b, x] = velocity[c]
            grad_x = [first_diff(lambda k, c=c: at(c, b, x + k)) for c in range(3)]
            for slot, (first, second) in enumerate(stress_pairs):
                comp = 3 + slot
                stress = stresses[slot]
                along_x = lambda k, comp=comp: at(comp, b, x + k)
                terms_ref[0, slot, b, x] = first_diff(lambda k, comp=comp: at(comp, b + k, x))
                terms_ref[1, slot, b, x] = velocity[0] * first_diff(along_x) + part_ref[0, slot, b, x]
                terms_ref[2, slot, b, x] = -(
                    stresses[pair_index(first, 0)] * grad_x[second]
                    + stresses[pair_index(second, 0)] * grad_x[first]
                    + part_ref[1, slot, b, x]
                )
                terms_ref[3, slot, b, x] = viscosity * (
                    second_diff(along_x, stress) + part_ref[2, slot, b, x]
                )


def finish_terms(fields, head, tail):
    _, bins_dev, planes, ny, nz = fields.shape
    from_left = lax.ppermute(fields, "rev", ring("rev", 1))
    from_right = lax.ppermute(fields, "rev", ring("rev", -1))
    from_prev = lax.ppermute(tail, "bin", ring("bin", 1))
    from_next = lax.ppermute(head, "bin", ring("bin", -1))
    cells = bins_dev * planes * ny * nz
    vmem = pl.BlockSpec(memory_space=pltpu.VMEM)
    part = pl.pallas_call(
        halo_free_kernel,
        out_shape=jax.ShapeDtypeStruct((3, 6, bins_dev, planes, ny, nz), jnp.float32),
        in_specs=[vmem],
        out_specs=vmem,
        compiler_params=pltpu.CompilerParams(vmem_limit_bytes=16 * 1024 * 1024),
        cost_estimate=pl.CostEstimate(
            flops=cells * 400, bytes_accessed=(9 + 18) * cells * 4, transcendentals=0
        ),
    )(fields)
    return pl.pallas_call(
        halo_kernel,
        out_shape=(
            jax.ShapeDtypeStruct((4, 6, bins_dev, planes, ny, nz), jnp.float32),
            jax.ShapeDtypeStruct((3, bins_dev, planes, ny, nz), jnp.float32),
        ),
        in_specs=[vmem] * 6,
        out_specs=(vmem, vmem),
        compiler_params=pltpu.CompilerParams(vmem_limit_bytes=16 * 1024 * 1024),
        cost_estimate=pl.CostEstimate(
            flops=cells * 300,
            bytes_accessed=(3 * fields.size + 2 * head.size + 45 * cells) * 4,
            transcendentals=0,
        ),
    )(fields, from_left, from_right, from_prev, from_next, part)


def shards(snapshots, phase_index):
    bins_dev = PHASES // lax.axis_size("bin")
    n_rev = lax.axis_size("rev")
    frames = snapshots[0]
    snaps, comps, nx, ny, nz = frames.shape
    planes = nx // n_rev
    by_dest = frames.reshape(snaps, comps, n_rev, planes, ny, nz)
    by_dest = jnp.transpose(by_dest, (2, 0, 1, 3, 4, 5)).reshape(n_rev, snaps * comps * planes, ny, nz)
    phase_row = jnp.pad(phase_index[0].astype(jnp.float32), (0, nz - snaps))
    phase_slab = jnp.broadcast_to(phase_row[None, None, None, :], (n_rev, 1, ny, nz))
    payload = jnp.concatenate([by_dest, phase_slab], axis=1)
    received = lax.all_to_all(payload, "rev", 0, 0, tiled=True)
    phases = received[:, -1, 0, :snaps].reshape(-1).astype(jnp.int32)
    local_bins = jnp.clip(phases - lax.axis_index("bin") * bins_dev, 0, bins_dev - 1)
    fields, head, tail = binned_fields(received, local_bins, bins_dev, planes)
    return finish_terms(fields, head, tail)


def solution(mesh):
    in_specs = (P("rev", "bin", None, None, None, None), P("rev", "bin"))
    out_specs = (P(None, None, "bin", "rev", None, None), P(None, "bin", "rev", None, None))
    return jax.shard_map(shards, mesh=mesh, in_specs=in_specs, out_specs=out_specs, check_vma=False)
```

```python
import jax
import jax.numpy as jnp
from jax import lax
from jax.experimental import pallas as pl
from jax.experimental.pallas import tpu as pltpu
from jax.sharding import PartitionSpec as P

PHASES = 256
HALO = 3

viscosity = 0.2
stress_pairs = ((0, 0), (0, 1), (0, 2), (1, 1), (1, 2), (2, 2))


def pair_index(first, second):
    low, high = (min(first, second), max(first, second))
    return stress_pairs.index((low, high))


def bin_kernel(bins_ref, x_ref, o_ref, head_ref, tail_ref, acc_ref):
    bins, _, planes = acc_ref.shape[0], acc_ref.shape[1], acc_ref.shape[2]
    per_src = (x_ref.shape[1] - 1) // (3 * planes)
    snaps = x_ref.shape[0] * per_src
    acc_ref[...] = jnp.zeros(acc_ref.shape, jnp.float32)

    def body(s, carry):
        b = bins_ref[s]
        src = s // per_src
        base = (s % per_src) * (3 * planes)
        for p in range(planes):
            u = x_ref[src, base + p]
            v = x_ref[src, base + planes + p]
            w = x_ref[src, base + 2 * planes + p]
            moments = (u, v, w, u * u, u * v, u * w, v * v, v * w, w * w)
            for k in range(9):
                acc_ref[b, k, p] = acc_ref[b, k, p] + moments[k]
        acc_ref[b, 9, 0] = acc_ref[b, 9, 0] + 1.0
        return carry

    lax.fori_loop(0, snaps, body, 0, unroll=2)

    for b in range(bins):
        count = acc_ref[b, 9, 0]
        for p in range(planes):
            vel = [acc_ref[b, c, p] / count for c in range(3)]
            for c in range(3):
                o_ref[c, b, p] = vel[c]
            for slot, (i, j) in enumerate(stress_pairs):
                stress = acc_ref[b, 3 + slot, p] / count - vel[i] * vel[j]
                o_ref[3 + slot, b, p] = stress
                if b < HALO:
                    head_ref[slot, b, p] = stress
                if b >= bins - HALO:
                    tail_ref[slot, b - (bins - HALO), p] = stress


def binned_fields(received, local_bins, bins, planes):
    n_src, rows, ny, nz = received.shape
    snaps = local_bins.shape[0]
    return pl.pallas_call(
        bin_kernel,
        out_shape=(
            jax.ShapeDtypeStruct((9, bins, planes, ny, nz), jnp.float32),
            jax.ShapeDtypeStruct((6, HALO, planes, ny, nz), jnp.float32),
            jax.ShapeDtypeStruct((6, HALO, planes, ny, nz), jnp.float32),
        ),
        in_specs=[pl.BlockSpec(memory_space=pltpu.SMEM), pl.BlockSpec(memory_space=pltpu.VMEM)],
        out_specs=(
            pl.BlockSpec(memory_space=pltpu.VMEM),
            pl.BlockSpec(memory_space=pltpu.VMEM),
            pl.BlockSpec(memory_space=pltpu.VMEM),
        ),
        scratch_shapes=[pltpu.VMEM((bins, 10, planes, ny, nz), jnp.float32)],
        compiler_params=pltpu.CompilerParams(vmem_limit_bytes=16 * 1024 * 1024),
        cost_estimate=pl.CostEstimate(
            flops=snaps * planes * ny * nz * 15,
            bytes_accessed=received.size * 4 + 9 * bins * planes * ny * nz * 4,
            transcendentals=0,
        ),
    )(local_bins, received)


def pack_kernel(phase_ref, x_ref, o_ref):
    snaps, comps, _, ny, nz = x_ref.shape
    n_dest, rows = o_ref.shape[0], o_ref.shape[1]
    planes = (rows - 1) // (snaps * comps)
    for d in range(n_dest):
        for s in range(snaps):
            for c in range(comps):
                o_ref[d, pl.ds((s * comps + c) * planes, planes)] = x_ref[s, c, pl.ds(d * planes, planes)]
    lane = lax.broadcasted_iota(jnp.int32, (ny, nz), 1)
    row = jnp.zeros((ny, nz), jnp.float32)
    for s in range(snaps):
        row = jnp.where(lane == s, phase_ref[s], row)
    for d in range(n_dest):
        o_ref[d, rows - 1] = row


def packed_payload(frames, phases, n_dest):
    snaps, comps, nx, ny, nz = frames.shape
    rows = snaps * comps * (nx // n_dest) + 1
    return pl.pallas_call(
        pack_kernel,
        out_shape=jax.ShapeDtypeStruct((n_dest, rows, ny, nz), jnp.float32),
        in_specs=[pl.BlockSpec(memory_space=pltpu.SMEM), pl.BlockSpec(memory_space=pltpu.VMEM)],
        out_specs=pl.BlockSpec(memory_space=pltpu.VMEM),
        compiler_params=pltpu.CompilerParams(vmem_limit_bytes=16 * 1024 * 1024),
        cost_estimate=pl.CostEstimate(
            flops=0, bytes_accessed=2 * frames.size * 4, transcendentals=0
        ),
    )(phases, frames)


def first_diff(shifted):
    return (
        0.75 * (shifted(1) - shifted(-1))
        - 0.15 * (shifted(2) - shifted(-2))
        + (shifted(3) - shifted(-3)) / 60.0
    )


def second_diff(shifted, centre):
    return (
        -49.0 / 18.0 * centre
        + 1.5 * (shifted(1) + shifted(-1))
        - 0.15 * (shifted(2) + shifted(-2))
        + (shifted(3) + shifted(-3)) / 90.0
    )


def ring(axis, step):
    count = lax.axis_size(axis)
    return [(i, (i + step) % count) for i in range(count)]


def halo_free_kernel(f_ref, part_ref):
    _, bins, planes, ny, nz = f_ref.shape

    def rolled(value, axis, size):
        table = {k: pltpu.roll(value, (-k) % size, axis) for k in (1, 2, 3, -1, -2, -3)}
        return lambda amount: table[amount]

    for b in range(bins):
        for x in range(planes):
            velocity = [f_ref[c, b, x] for c in range(3)]
            stresses = [f_ref[3 + m, b, x] for m in range(6)]
            grad_u = [
                [None, first_diff(rolled(velocity[c], 0, ny)), first_diff(rolled(velocity[c], 1, nz))]
                for c in range(3)
            ]
            for slot, (first, second) in enumerate(stress_pairs):
                stress = stresses[slot]
                along_y = rolled(stress, 0, ny)
                along_z = rolled(stress, 1, nz)
                part_ref[0, slot, b, x] = velocity[1] * first_diff(along_y) + velocity[2] * first_diff(along_z)
                summed = None
                for dim in (1, 2):
                    pair_sum = (
                        stresses[pair_index(first, dim)] * grad_u[second][dim]
                        + stresses[pair_index(second, dim)] * grad_u[first][dim]
                    )
                    summed = pair_sum if summed is None else summed + pair_sum
                part_ref[1, slot, b, x] = summed
                part_ref[2, slot, b, x] = second_diff(along_y, stress) + second_diff(along_z, stress)


def halo_kernel(f_ref, fl_ref, fr_ref, rp_ref, rn_ref, part_ref, terms_ref, vel_ref):
    _, bins, planes, ny, nz = f_ref.shape

    def at(comp, b, x):
        if 0 <= x < planes:
            if 0 <= b < bins:
                return f_ref[comp, b, x]
            if b < 0:
                return rp_ref[comp - 3, b + HALO, x]
            return rn_ref[comp - 3, b - bins, x]
        if x < 0:
            return fl_ref[comp, b, x + planes]
        return fr_ref[comp, b, x - planes]

    for b in range(bins):
        for x in range(planes):
            velocity = [f_ref[c, b, x] for c in range(3)]
            stresses = [f_ref[3 + m, b, x] for m in range(6)]
            for c in range(3):
                vel_ref[c, b, x] = velocity[c]
            grad_x = [first_diff(lambda k, c=c: at(c, b, x + k)) for c in range(3)]
            for slot, (first, second) in enumerate(stress_pairs):
                comp = 3 + slot
                stress = stresses[slot]
                along_x = lambda k, comp=comp: at(comp, b, x + k)
                terms_ref[0, slot, b, x] = first_diff(lambda k, comp=comp: at(comp, b + k, x))
                terms_ref[1, slot, b, x] = velocity[0] * first_diff(along_x) + part_ref[0, slot, b, x]
                terms_ref[2, slot, b, x] = -(
                    stresses[pair_index(first, 0)] * grad_x[second]
                    + stresses[pair_index(second, 0)] * grad_x[first]
                    + part_ref[1, slot, b, x]
                )
                terms_ref[3, slot, b, x] = viscosity * (
                    second_diff(along_x, stress) + part_ref[2, slot, b, x]
                )


def finish_terms(fields, head, tail):
    _, bins_dev, planes, ny, nz = fields.shape
    from_left = lax.ppermute(fields, "rev", ring("rev", 1))
    from_right = lax.ppermute(fields, "rev", ring("rev", -1))
    from_prev = lax.ppermute(tail, "bin", ring("bin", 1))
    from_next = lax.ppermute(head, "bin", ring("bin", -1))
    cells = bins_dev * planes * ny * nz
    vmem = pl.BlockSpec(memory_space=pltpu.VMEM)
    part = pl.pallas_call(
        halo_free_kernel,
        out_shape=jax.ShapeDtypeStruct((3, 6, bins_dev, planes, ny, nz), jnp.float32),
        in_specs=[vmem],
        out_specs=vmem,
        compiler_params=pltpu.CompilerParams(vmem_limit_bytes=16 * 1024 * 1024),
        cost_estimate=pl.CostEstimate(
            flops=cells * 400, bytes_accessed=(9 + 18) * cells * 4, transcendentals=0
        ),
    )(fields)
    return pl.pallas_call(
        halo_kernel,
        out_shape=(
            jax.ShapeDtypeStruct((4, 6, bins_dev, planes, ny, nz), jnp.float32),
            jax.ShapeDtypeStruct((3, bins_dev, planes, ny, nz), jnp.float32),
        ),
        in_specs=[vmem] * 6,
        out_specs=(vmem, vmem),
        compiler_params=pltpu.CompilerParams(vmem_limit_bytes=16 * 1024 * 1024),
        cost_estimate=pl.CostEstimate(
            flops=cells * 300,
            bytes_accessed=(3 * fields.size + 2 * head.size + 45 * cells) * 4,
            transcendentals=0,
        ),
    )(fields, from_left, from_right, from_prev, from_next, part)


def shards(snapshots, phase_index):
    bins_dev = PHASES // lax.axis_size("bin")
    n_rev = lax.axis_size("rev")
    frames = snapshots[0]
    snaps, comps, nx, ny, nz = frames.shape
    planes = nx // n_rev
    payload = packed_payload(frames, phase_index[0].astype(jnp.float32), n_rev)
    received = lax.all_to_all(payload, "rev", 0, 0, tiled=True)
    phases = received[:, -1, 0, :snaps].reshape(-1).astype(jnp.int32)
    local_bins = jnp.clip(phases - lax.axis_index("bin") * bins_dev, 0, bins_dev - 1)
    fields, head, tail = binned_fields(received, local_bins, bins_dev, planes)
    return finish_terms(fields, head, tail)


def solution(mesh):
    in_specs = (P("rev", "bin", None, None, None, None), P("rev", "bin"))
    out_specs = (P(None, None, "bin", "rev", None, None), P(None, "bin", "rev", None, None))
    return jax.shard_map(shards, mesh=mesh, in_specs=in_specs, out_specs=out_specs, check_vma=False)
```

```python
import jax
import jax.numpy as jnp
from jax import lax
from jax.experimental import pallas as pl
from jax.experimental.pallas import tpu as pltpu
from jax.sharding import PartitionSpec as P

PHASES = 256
HALO = 3

viscosity = 0.2
stress_pairs = ((0, 0), (0, 1), (0, 2), (1, 1), (1, 2), (2, 2))


def pair_index(first, second):
    low, high = (min(first, second), max(first, second))
    return stress_pairs.index((low, high))


def bin_kernel(bins_ref, x_ref, o_ref, head_ref, tail_ref, acc_ref):
    bins, _, planes = acc_ref.shape[0], acc_ref.shape[1], acc_ref.shape[2]
    per_src = (x_ref.shape[1] - 1) // (3 * planes)
    snaps = x_ref.shape[0] * per_src
    acc_ref[...] = jnp.zeros(acc_ref.shape, jnp.float32)

    def body(s, carry):
        b = bins_ref[s]
        src = s // per_src
        base = (s % per_src) * (3 * planes)
        for p in range(planes):
            u = x_ref[src, base + p]
            v = x_ref[src, base + planes + p]
            w = x_ref[src, base + 2 * planes + p]
            moments = (u, v, w, u * u, u * v, u * w, v * v, v * w, w * w)
            for k in range(9):
                acc_ref[b, k, p] = acc_ref[b, k, p] + moments[k]
        acc_ref[b, 9, 0] = acc_ref[b, 9, 0] + 1.0
        return carry

    lax.fori_loop(0, snaps, body, 0, unroll=2)

    for b in range(bins):
        count = acc_ref[b, 9, 0]
        for p in range(planes):
            vel = [acc_ref[b, c, p] / count for c in range(3)]
            for c in range(3):
                o_ref[c, b, p] = vel[c]
            for slot, (i, j) in enumerate(stress_pairs):
                stress = acc_ref[b, 3 + slot, p] / count - vel[i] * vel[j]
                o_ref[3 + slot, b, p] = stress
                if b < HALO:
                    head_ref[slot, b, p] = stress
                if b >= bins - HALO:
                    tail_ref[slot, b - (bins - HALO), p] = stress


def binned_fields(received, local_bins, bins, planes):
    n_src, rows, ny, nz = received.shape
    snaps = local_bins.shape[0]
    return pl.pallas_call(
        bin_kernel,
        out_shape=(
            jax.ShapeDtypeStruct((9, bins, planes, ny, nz), jnp.float32),
            jax.ShapeDtypeStruct((6, HALO, planes, ny, nz), jnp.float32),
            jax.ShapeDtypeStruct((6, HALO, planes, ny, nz), jnp.float32),
        ),
        in_specs=[pl.BlockSpec(memory_space=pltpu.SMEM), pl.BlockSpec(memory_space=pltpu.VMEM)],
        out_specs=(
            pl.BlockSpec(memory_space=pltpu.VMEM),
            pl.BlockSpec(memory_space=pltpu.VMEM),
            pl.BlockSpec(memory_space=pltpu.VMEM),
        ),
        scratch_shapes=[pltpu.VMEM((bins, 10, planes, ny, nz), jnp.float32)],
        compiler_params=pltpu.CompilerParams(vmem_limit_bytes=16 * 1024 * 1024),
        cost_estimate=pl.CostEstimate(
            flops=snaps * planes * ny * nz * 15,
            bytes_accessed=received.size * 4 + 9 * bins * planes * ny * nz * 4,
            transcendentals=0,
        ),
    )(local_bins, received)


def first_diff(shifted):
    return (
        0.75 * (shifted(1) - shifted(-1))
        - 0.15 * (shifted(2) - shifted(-2))
        + (shifted(3) - shifted(-3)) / 60.0
    )


def second_diff(shifted, centre):
    return (
        -49.0 / 18.0 * centre
        + 1.5 * (shifted(1) + shifted(-1))
        - 0.15 * (shifted(2) + shifted(-2))
        + (shifted(3) + shifted(-3)) / 90.0
    )


def ring(axis, step):
    count = lax.axis_size(axis)
    return [(i, (i + step) % count) for i in range(count)]


def halo_free_kernel(f_ref, part_ref, vel_ref):
    _, bins, planes, ny, nz = f_ref.shape

    def rolled(value, axis, size):
        table = {k: pltpu.roll(value, (-k) % size, axis) for k in (1, 2, 3, -1, -2, -3)}
        return lambda amount: table[amount]

    for b in range(bins):
        for x in range(planes):
            velocity = [f_ref[c, b, x] for c in range(3)]
            stresses = [f_ref[3 + m, b, x] for m in range(6)]
            for c in range(3):
                vel_ref[c, b, x] = velocity[c]
            grad_u = [
                [None, first_diff(rolled(velocity[c], 0, ny)), first_diff(rolled(velocity[c], 1, nz))]
                for c in range(3)
            ]
            for slot, (first, second) in enumerate(stress_pairs):
                stress = stresses[slot]
                along_y = rolled(stress, 0, ny)
                along_z = rolled(stress, 1, nz)
                part_ref[0, slot, b, x] = velocity[1] * first_diff(along_y) + velocity[2] * first_diff(along_z)
                summed = None
                for dim in (1, 2):
                    pair_sum = (
                        stresses[pair_index(first, dim)] * grad_u[second][dim]
                        + stresses[pair_index(second, dim)] * grad_u[first][dim]
                    )
                    summed = pair_sum if summed is None else summed + pair_sum
                part_ref[1, slot, b, x] = summed
                part_ref[2, slot, b, x] = second_diff(along_y, stress) + second_diff(along_z, stress)


def halo_kernel(f_ref, fl_ref, fr_ref, rp_ref, rn_ref, part_ref, terms_ref):
    _, bins, planes, ny, nz = f_ref.shape

    def at(comp, b, x):
        if 0 <= x < planes:
            if 0 <= b < bins:
                return f_ref[comp, b, x]
            if b < 0:
                return rp_ref[comp - 3, b + HALO, x]
            return rn_ref[comp - 3, b - bins, x]
        if x < 0:
            return fl_ref[comp, b, x + planes]
        return fr_ref[comp, b, x - planes]

    for b in range(bins):
        for x in range(planes):
            velocity = [f_ref[c, b, x] for c in range(3)]
            stresses = [f_ref[3 + m, b, x] for m in range(6)]
            grad_x = [first_diff(lambda k, c=c: at(c, b, x + k)) for c in range(3)]
            for slot, (first, second) in enumerate(stress_pairs):
                comp = 3 + slot
                stress = stresses[slot]
                along_x = lambda k, comp=comp: at(comp, b, x + k)
                terms_ref[0, slot, b, x] = first_diff(lambda k, comp=comp: at(comp, b + k, x))
                terms_ref[1, slot, b, x] = velocity[0] * first_diff(along_x) + part_ref[0, slot, b, x]
                terms_ref[2, slot, b, x] = -(
                    stresses[pair_index(first, 0)] * grad_x[second]
                    + stresses[pair_index(second, 0)] * grad_x[first]
                    + part_ref[1, slot, b, x]
                )
                terms_ref[3, slot, b, x] = viscosity * (
                    second_diff(along_x, stress) + part_ref[2, slot, b, x]
                )


def finish_terms(fields, head, tail):
    _, bins_dev, planes, ny, nz = fields.shape
    from_left = lax.ppermute(fields, "rev", ring("rev", 1))
    from_right = lax.ppermute(fields, "rev", ring("rev", -1))
    from_prev = lax.ppermute(tail, "bin", ring("bin", 1))
    from_next = lax.ppermute(head, "bin", ring("bin", -1))
    cells = bins_dev * planes * ny * nz
    vmem = pl.BlockSpec(memory_space=pltpu.VMEM)
    part, mean_velocity = pl.pallas_call(
        halo_free_kernel,
        out_shape=(
            jax.ShapeDtypeStruct((3, 6, bins_dev, planes, ny, nz), jnp.float32),
            jax.ShapeDtypeStruct((3, bins_dev, planes, ny, nz), jnp.float32),
        ),
        in_specs=[vmem],
        out_specs=(vmem, vmem),
        compiler_params=pltpu.CompilerParams(vmem_limit_bytes=16 * 1024 * 1024),
        cost_estimate=pl.CostEstimate(
            flops=cells * 400, bytes_accessed=(9 + 18) * cells * 4, transcendentals=0
        ),
    )(fields)
    terms = pl.pallas_call(
        halo_kernel,
        out_shape=jax.ShapeDtypeStruct((4, 6, bins_dev, planes, ny, nz), jnp.float32),
        in_specs=[vmem] * 6,
        out_specs=vmem,
        compiler_params=pltpu.CompilerParams(vmem_limit_bytes=16 * 1024 * 1024),
        cost_estimate=pl.CostEstimate(
            flops=cells * 300,
            bytes_accessed=(3 * fields.size + 2 * head.size + 45 * cells) * 4,
            transcendentals=0,
        ),
    )(fields, from_left, from_right, from_prev, from_next, part)
    return terms, mean_velocity


def shards(snapshots, phase_index):
    bins_dev = PHASES // lax.axis_size("bin")
    n_rev = lax.axis_size("rev")
    frames = snapshots[0]
    snaps, comps, nx, ny, nz = frames.shape
    planes = nx // n_rev
    by_dest = frames.reshape(snaps, comps, n_rev, planes, ny, nz)
    by_dest = jnp.transpose(by_dest, (2, 0, 1, 3, 4, 5)).reshape(n_rev, snaps * comps * planes, ny, nz)
    phase_row = jnp.pad(phase_index[0].astype(jnp.float32), (0, nz - snaps))
    phase_slab = jnp.broadcast_to(phase_row[None, None, None, :], (n_rev, 1, ny, nz))
    payload = jnp.concatenate([by_dest, phase_slab], axis=1)
    received = lax.all_to_all(payload, "rev", 0, 0, tiled=True)
    phases = received[:, -1, 0, :snaps].reshape(-1).astype(jnp.int32)
    local_bins = jnp.clip(phases - lax.axis_index("bin") * bins_dev, 0, bins_dev - 1)
    fields, head, tail = binned_fields(received, local_bins, bins_dev, planes)
    return finish_terms(fields, head, tail)


def solution(mesh):
    in_specs = (P("rev", "bin", None, None, None, None), P("rev", "bin"))
    out_specs = (P(None, None, "bin", "rev", None, None), P(None, "bin", "rev", None, None))
    return jax.shard_map(shards, mesh=mesh, in_specs=in_specs, out_specs=out_specs, check_vma=False)
```

```python
import jax
import jax.numpy as jnp
from jax import lax
from jax.experimental import pallas as pl
from jax.experimental.pallas import tpu as pltpu
from jax.sharding import PartitionSpec as P

PHASES = 256
HALO = 3

viscosity = 0.2
stress_pairs = ((0, 0), (0, 1), (0, 2), (1, 1), (1, 2), (2, 2))


def pair_index(first, second):
    low, high = (min(first, second), max(first, second))
    return stress_pairs.index((low, high))


def bin_kernel(bins_ref, x_ref, o_ref, head_ref, tail_ref, acc_ref):
    bins, _, planes = acc_ref.shape[0], acc_ref.shape[1], acc_ref.shape[2]
    per_src = (x_ref.shape[1] - 1) // (3 * planes)
    snaps = x_ref.shape[0] * per_src
    acc_ref[...] = jnp.zeros(acc_ref.shape, jnp.float32)

    def body(s, carry):
        b = bins_ref[s]
        src = s // per_src
        base = (s % per_src) * (3 * planes)
        for p in range(planes):
            u = x_ref[src, base + p]
            v = x_ref[src, base + planes + p]
            w = x_ref[src, base + 2 * planes + p]
            moments = (u, v, w, u * u, u * v, u * w, v * v, v * w, w * w)
            for k in range(9):
                acc_ref[b, k, p] = acc_ref[b, k, p] + moments[k]
        acc_ref[b, 9, 0] = acc_ref[b, 9, 0] + 1.0
        return carry

    lax.fori_loop(0, snaps, body, 0, unroll=4)

    for b in range(bins):
        count = acc_ref[b, 9, 0]
        for p in range(planes):
            vel = [acc_ref[b, c, p] / count for c in range(3)]
            for c in range(3):
                o_ref[c, b, p] = vel[c]
            for slot, (i, j) in enumerate(stress_pairs):
                stress = acc_ref[b, 3 + slot, p] / count - vel[i] * vel[j]
                o_ref[3 + slot, b, p] = stress
                if b < HALO:
                    head_ref[slot, b, p] = stress
                if b >= bins - HALO:
                    tail_ref[slot, b - (bins - HALO), p] = stress


def binned_fields(received, local_bins, bins, planes):
    n_src, rows, ny, nz = received.shape
    snaps = local_bins.shape[0]
    return pl.pallas_call(
        bin_kernel,
        out_shape=(
            jax.ShapeDtypeStruct((9, bins, planes, ny, nz), jnp.float32),
            jax.ShapeDtypeStruct((6, HALO, planes, ny, nz), jnp.float32),
            jax.ShapeDtypeStruct((6, HALO, planes, ny, nz), jnp.float32),
        ),
        in_specs=[pl.BlockSpec(memory_space=pltpu.SMEM), pl.BlockSpec(memory_space=pltpu.VMEM)],
        out_specs=(
            pl.BlockSpec(memory_space=pltpu.VMEM),
            pl.BlockSpec(memory_space=pltpu.VMEM),
            pl.BlockSpec(memory_space=pltpu.VMEM),
        ),
        scratch_shapes=[pltpu.VMEM((bins, 10, planes, ny, nz), jnp.float32)],
        compiler_params=pltpu.CompilerParams(vmem_limit_bytes=16 * 1024 * 1024),
        cost_estimate=pl.CostEstimate(
            flops=snaps * planes * ny * nz * 15,
            bytes_accessed=received.size * 4 + 9 * bins * planes * ny * nz * 4,
            transcendentals=0,
        ),
    )(local_bins, received)


def first_diff(shifted):
    return (
        0.75 * (shifted(1) - shifted(-1))
        - 0.15 * (shifted(2) - shifted(-2))
        + (shifted(3) - shifted(-3)) / 60.0
    )


def second_diff(shifted, centre):
    return (
        -49.0 / 18.0 * centre
        + 1.5 * (shifted(1) + shifted(-1))
        - 0.15 * (shifted(2) + shifted(-2))
        + (shifted(3) + shifted(-3)) / 90.0
    )


def ring(axis, step):
    count = lax.axis_size(axis)
    return [(i, (i + step) % count) for i in range(count)]


def halo_free_kernel(f_ref, part_ref):
    _, bins, planes, ny, nz = f_ref.shape

    def rolled(value, axis, size):
        table = {k: pltpu.roll(value, (-k) % size, axis) for k in (1, 2, 3, -1, -2, -3)}
        return lambda amount: table[amount]

    for b in range(bins):
        for x in range(planes):
            velocity = [f_ref[c, b, x] for c in range(3)]
            stresses = [f_ref[3 + m, b, x] for m in range(6)]
            grad_u = [
                [None, first_diff(rolled(velocity[c], 0, ny)), first_diff(rolled(velocity[c], 1, nz))]
                for c in range(3)
            ]
            for slot, (first, second) in enumerate(stress_pairs):
                stress = stresses[slot]
                along_y = rolled(stress, 0, ny)
                along_z = rolled(stress, 1, nz)
                part_ref[0, slot, b, x] = velocity[1] * first_diff(along_y) + velocity[2] * first_diff(along_z)
                summed = None
                for dim in (1, 2):
                    pair_sum = (
                        stresses[pair_index(first, dim)] * grad_u[second][dim]
                        + stresses[pair_index(second, dim)] * grad_u[first][dim]
                    )
                    summed = pair_sum if summed is None else summed + pair_sum
                part_ref[1, slot, b, x] = summed
                part_ref[2, slot, b, x] = second_diff(along_y, stress) + second_diff(along_z, stress)


def halo_kernel(f_ref, fl_ref, fr_ref, rp_ref, rn_ref, part_ref, terms_ref, vel_ref):
    _, bins, planes, ny, nz = f_ref.shape

    def at(comp, b, x):
        if 0 <= x < planes:
            if 0 <= b < bins:
                return f_ref[comp, b, x]
            if b < 0:
                return rp_ref[comp - 3, b + HALO, x]
            return rn_ref[comp - 3, b - bins, x]
        if x < 0:
            return fl_ref[comp, b, x + planes]
        return fr_ref[comp, b, x - planes]

    for b in range(bins):
        for x in range(planes):
            velocity = [f_ref[c, b, x] for c in range(3)]
            stresses = [f_ref[3 + m, b, x] for m in range(6)]
            for c in range(3):
                vel_ref[c, b, x] = velocity[c]
            grad_x = [first_diff(lambda k, c=c: at(c, b, x + k)) for c in range(3)]
            for slot, (first, second) in enumerate(stress_pairs):
                comp = 3 + slot
                stress = stresses[slot]
                along_x = lambda k, comp=comp: at(comp, b, x + k)
                terms_ref[0, slot, b, x] = first_diff(lambda k, comp=comp: at(comp, b + k, x))
                terms_ref[1, slot, b, x] = velocity[0] * first_diff(along_x) + part_ref[0, slot, b, x]
                terms_ref[2, slot, b, x] = -(
                    stresses[pair_index(first, 0)] * grad_x[second]
                    + stresses[pair_index(second, 0)] * grad_x[first]
                    + part_ref[1, slot, b, x]
                )
                terms_ref[3, slot, b, x] = viscosity * (
                    second_diff(along_x, stress) + part_ref[2, slot, b, x]
                )


def finish_terms(fields, head, tail):
    _, bins_dev, planes, ny, nz = fields.shape
    from_left = lax.ppermute(fields, "rev", ring("rev", 1))
    from_right = lax.ppermute(fields, "rev", ring("rev", -1))
    from_prev = lax.ppermute(tail, "bin", ring("bin", 1))
    from_next = lax.ppermute(head, "bin", ring("bin", -1))
    cells = bins_dev * planes * ny * nz
    vmem = pl.BlockSpec(memory_space=pltpu.VMEM)
    part = pl.pallas_call(
        halo_free_kernel,
        out_shape=jax.ShapeDtypeStruct((3, 6, bins_dev, planes, ny, nz), jnp.float32),
        in_specs=[vmem],
        out_specs=vmem,
        compiler_params=pltpu.CompilerParams(vmem_limit_bytes=16 * 1024 * 1024),
        cost_estimate=pl.CostEstimate(
            flops=cells * 400, bytes_accessed=(9 + 18) * cells * 4, transcendentals=0
        ),
    )(fields)
    return pl.pallas_call(
        halo_kernel,
        out_shape=(
            jax.ShapeDtypeStruct((4, 6, bins_dev, planes, ny, nz), jnp.float32),
            jax.ShapeDtypeStruct((3, bins_dev, planes, ny, nz), jnp.float32),
        ),
        in_specs=[vmem] * 6,
        out_specs=(vmem, vmem),
        compiler_params=pltpu.CompilerParams(vmem_limit_bytes=16 * 1024 * 1024),
        cost_estimate=pl.CostEstimate(
            flops=cells * 300,
            bytes_accessed=(3 * fields.size + 2 * head.size + 45 * cells) * 4,
            transcendentals=0,
        ),
    )(fields, from_left, from_right, from_prev, from_next, part)


def shards(snapshots, phase_index):
    bins_dev = PHASES // lax.axis_size("bin")
    n_rev = lax.axis_size("rev")
    frames = snapshots[0]
    snaps, comps, nx, ny, nz = frames.shape
    planes = nx // n_rev
    by_dest = frames.reshape(snaps, comps, n_rev, planes, ny, nz)
    by_dest = jnp.transpose(by_dest, (2, 0, 1, 3, 4, 5)).reshape(n_rev, snaps * comps * planes, ny, nz)
    phase_row = jnp.pad(phase_index[0].astype(jnp.float32), (0, nz - snaps))
    phase_slab = jnp.broadcast_to(phase_row[None, None, None, :], (n_rev, 1, ny, nz))
    payload = jnp.concatenate([by_dest, phase_slab], axis=1)
    received = lax.all_to_all(payload, "rev", 0, 0, tiled=True)
    phases = received[:, -1, 0, :snaps].reshape(-1).astype(jnp.int32)
    local_bins = jnp.clip(phases - lax.axis_index("bin") * bins_dev, 0, bins_dev - 1)
    fields, head, tail = binned_fields(received, local_bins, bins_dev, planes)
    return finish_terms(fields, head, tail)


def solution(mesh):
    in_specs = (P("rev", "bin", None, None, None, None), P("rev", "bin"))
    out_specs = (P(None, None, "bin", "rev", None, None), P(None, "bin", "rev", None, None))
    return jax.shard_map(shards, mesh=mesh, in_specs=in_specs, out_specs=out_specs, check_vma=False)
```
